512 devices in a mesh: patch: 8 (over y, core), au: 4 (over z_lo), vert: 16 (over x, z_hi).
Axes of the slice: x: 4, y: 4, z: 16 (z_hi: 4, z_lo: 4; z = z_hi * 4 + z_lo), core: 2. Of those that a mesh axis runs over, the one named last changes fastest.
Arguments:
- fields: bfloat16 [8, 8, 32, 256, 512], P('patch', None, None, 'vert', 'au'), may hold values from -6 to 6
- coef_u: float32 [3, 512], P(None, 'au'), may hold values from 0.1 to 0.3
- coef_v: float32 [3, 256], P(None, 'vert'), may hold values from 0.1 to 0.3
- coef_w: float32 [3, 32], replicated, may hold values from 0.1 to 0.3
- orient: int32 [8, 2], replicated, may hold values from 0 to 1
- link: int32 [8], replicated, may hold values from 1 to 4
Outputs:
- design: float32 [8, 4, 32, 64], P('patch', None, 'vert', 'au')
The draws below stay inside these ranges and needn't reach their ends.
All inputs are finite; a program needn't handle non-finite values.
Results may differ from the reference program's by a relative error of at most 0.0003.
Values may be sent and summed in bfloat16 or wider, within the bound.
No kernel may reach another device: no remote copies, remote signals or barrier semaphores. Data moves between devices by JAX's collectives and lax.ppermute only.
A program may use at most 128 MiB of HBM per device.

```python
import jax
import jax.numpy as jnp
from jax import lax

NW = 32
RATIO = 8
NPATCH = 8
NU = 512
NV = 256
DU = 64
DV = 32
DW = 4


def place_ends(array, rng, low, largest):
    longest = array.shape.index(max(array.shape))
    spots = []
    for shift in (0, 1):
        where = [jax.random.randint(jax.random.fold_in(rng, axis), (), 0, length) for axis, length in enumerate(array.shape)]
        where[longest] = (where[longest] + shift) % array.shape[longest]
        spots.append(tuple(where))
    return array.at[spots[0]].set(low).at[spots[1]].set(largest)


def block_levels(own_key, shape, split, smallest, high):
    level = 1.0
    for axis_at, parts in split:
        heights = jax.random.uniform(jax.random.fold_in(jax.random.fold_in(own_key, 6), axis_at), (parts,), jnp.float32, smallest / len(split), high / len(split))
        level = level * jnp.repeat(jnp.exp(heights), shape[axis_at] // parts).reshape((-1,) + (1,) * (len(shape) - 1 - axis_at))
    return level


def noise(key, dims, width, most, shards=(), dtype=jnp.bfloat16):
    values = jax.random.normal(key, dims, jnp.float32) * width
    if len(shards) > 0:
        values = block_levels(key, dims, shards, -0.22, 0.18) * values
    return jnp.clip(values, min=-most, max=most).astype(dtype)


def setup_inputs(seed: int = 0) -> dict:
    keys = jax.random.split(jax.random.key(seed), 7)
    fields = noise(keys[0], (NPATCH, 8, NW, NV, NU), 1.0, 6.0, ((0, 8), (3, 16), (4, 4)))
    coef_u = jnp.clip(0.1 + 0.20000001043081284 * jax.random.uniform(keys[1], (3, NU), jnp.float32) ** block_levels(keys[1], (3, NU), ((1, 4),), -0.2, 0.2), 0.1, 0.3)
    coef_v = jnp.clip(0.1 + 0.20000001043081284 * jax.random.uniform(keys[2], (3, NV), jnp.float32) ** block_levels(keys[2], (3, NV), ((1, 16),), -0.2, 0.2), 0.1, 0.3)
    coef_w = jnp.clip(jax.random.uniform(keys[3], (3, NW), jnp.float32, 0.1, 0.3), 0.1, 0.3)
    orient = place_ends(jax.random.randint(keys[4], (NPATCH, 2), 0, 2), jax.random.fold_in(keys[4], 1), 0, 1).astype(jnp.int32)
    link = place_ends(jax.random.randint(keys[5], (NPATCH,), 1, 5), jax.random.fold_in(keys[5], 1), 1, 4).astype(jnp.int32)
    return dict(fields=fields, coef_u=coef_u, coef_v=coef_v, coef_w=coef_w, orient=orient, link=link)


def difference(field_in, direction):
    length = field_in.shape[direction]
    widths = [(0, 0)] * field_in.ndim
    widths[direction] = (2, 2)
    padded = jnp.pad(field_in, widths)

    def shifted(offset):
        return lax.slice_in_dim(padded, 2 + offset, 2 + offset + length, axis=direction)

    return (8.0 * (shifted(1) - shifted(-1)) - (shifted(2) - shifted(-2))) / 12.0


def smooth_axis(field_in, direction):
    length = field_in.shape[direction]
    widths = [(0, 0)] * field_in.ndim
    widths[direction] = (1, 1)
    padded = jnp.pad(field_in, widths)

    def shifted(offset):
        return lax.slice_in_dim(padded, 1 + offset, 1 + offset + length, axis=direction)

    return (shifted(-1) + 4.0 * shifted(0) + shifted(1)) / 6.0


def patch_density(patch_block):
    floats_in = patch_block.astype(jnp.float32)
    product_sum = jnp.zeros(floats_in.shape[1:], jnp.float32)
    div_flow = jnp.zeros(floats_in.shape[1:], jnp.float32)
    div_adjoint = jnp.zeros(floats_in.shape[1:], jnp.float32)
    for direction in (1, 2, 3):
        slopes = difference(floats_in, direction)
        component = 3 - direction
        for k in range(3):
            product_sum = product_sum + slopes[k] * slopes[4 + k]
        div_flow = div_flow + slopes[component]
        div_adjoint = div_adjoint + slopes[4 + component]
    return product_sum - floats_in[3] * div_adjoint - floats_in[7] * div_flow


def band_matrix(coef_in, columns, offset):
    row_count = coef_in.shape[1]
    target = (jnp.arange(row_count) // RATIO)[:, None] + offset
    column = jnp.arange(columns)[None, :]
    result = jnp.zeros((row_count, columns), jnp.float32)
    for d in range(3):
        result = result + jnp.where(column == target + (d - 1), coef_in[d][:, None], 0.0)
    return result


def reference(fields, coef_u, coef_v, coef_w, orient, link):
    highest = lax.Precision.HIGHEST
    mat_u = band_matrix(coef_u, DU, 0)
    mat_v = band_matrix(coef_v, DV, 0)
    mat_w = band_matrix(coef_w, DW, 0)

    def one_patch(patch_block):
        density = patch_density(patch_block)
        smooth = smooth_axis(smooth_axis(smooth_axis(density, 0), 1), 2)
        reduced = jnp.einsum("wvu,wa->avu", smooth, mat_w, precision=highest)
        reduced = jnp.einsum("avu,vb->abu", reduced, mat_v, precision=highest)
        return jnp.einsum("abu,uc->abc", reduced, mat_u, precision=highest)

    partial_value = lax.map(one_patch, fields)
    layers_w = partial_value.shape[1]
    out_index = jnp.where(orient[:, 0] == 1, 0, layers_w - 1).astype(jnp.int32)
    in_index = jnp.where(orient[:, 1] == 1, layers_w - 1, 0).astype(jnp.int32)
    layer_ids = jnp.arange(layers_w).astype(jnp.int32)
    out_mask = (layer_ids[None, :] == out_index[:, None]).astype(jnp.float32)
    in_mask = (layer_ids[None, :] == in_index[:, None]).astype(jnp.float32)
    out_face = jnp.sum(out_mask[:, :, None, None] * partial_value, axis=1)
    in_face = jnp.sum(in_mask[:, :, None, None] * partial_value, axis=1)
    gate_on = link.astype(jnp.float32)[:, None, None]
    from_before = jnp.roll(out_face * gate_on, 1, axis=0)
    from_after = jnp.roll(in_face, -1, axis=0) * gate_on
    design = partial_value + in_mask[:, :, None, None] * from_before[:, None] + out_mask[:, :, None, None] * from_after[:, None]
    return design
```

```python
import jax
import jax.numpy as jnp
from jax import lax
from jax.sharding import PartitionSpec as P

RATIO = 8


def with_halo(block, sides, width):
    for axis, dim in sides:
        count = lax.axis_size(axis)
        forward = [(i, i + 1) for i in range(count - 1)]
        backward = [(target, source) for source, target in forward]
        low = lax.ppermute(
            lax.slice_in_dim(block, block.shape[dim] - width, None, axis=dim), axis, forward
        )
        high = lax.ppermute(lax.slice_in_dim(block, 0, width, axis=dim), axis, backward)
        block = jnp.concatenate([low, block, high], axis=dim)
    return block


def from_behind(block, axis, distance):
    devices = range(lax.axis_size(axis))
    route = [((i - distance) % len(devices), i) for i in devices]
    return lax.ppermute(block, axis, route)


def field_density(extended, width, reach, layers_w, rows_v, rows_u):
    padded = jnp.pad(extended, ((0, 0), (2, 2), (0, 0), (0, 0)))
    channels = extended.shape[0]
    anchor = (0, 2, width - reach, width - reach)
    extent = (channels, layers_w, rows_v + 2 * reach, rows_u + 2 * reach)

    def shifted(direction, offset):
        corner_at = list(anchor)
        corner_at[direction] = corner_at[direction] + offset
        limit_at = tuple((b + s for b, s in zip(corner_at, extent)))
        return lax.slice(padded, tuple(corner_at), limit_at).astype(jnp.float32)

    centre = shifted(1, 0)
    product_sum = jnp.zeros(extent[1:], jnp.float32)
    div_flow = jnp.zeros(extent[1:], jnp.float32)
    div_adjoint = jnp.zeros(extent[1:], jnp.float32)
    for direction in (1, 2, 3):
        slopes = (
            8.0 * (shifted(direction, 1) - shifted(direction, -1))
            - (shifted(direction, 2) - shifted(direction, -2))
        ) / 12.0
        component = 3 - direction
        for k in range(3):
            product_sum = product_sum + slopes[k] * slopes[4 + k]
        div_flow = div_flow + slopes[component]
        div_adjoint = div_adjoint + slopes[4 + component]
    return product_sum - centre[3] * div_adjoint - centre[7] * div_flow


def blur(widened):
    padded = jnp.pad(widened, ((1, 1), (0, 0), (0, 0)))
    along_w = (padded[:-2] + 4.0 * padded[1:-1] + padded[2:]) / 6.0
    along_v = (along_w[:, :-2] + 4.0 * along_w[:, 1:-1] + along_w[:, 2:]) / 6.0
    return (along_v[:, :, :-2] + 4.0 * along_v[:, :, 1:-1] + along_v[:, :, 2:]) / 6.0


def band_matrix(coef_in, columns, offset):
    row_count = coef_in.shape[1]
    target = (jnp.arange(row_count) // RATIO)[:, None] + offset
    column = jnp.arange(columns)[None, :]
    result = jnp.zeros((row_count, columns), jnp.float32)
    for d in range(3):
        result = result + jnp.where(column == target + (d - 1), coef_in[d][:, None], 0.0)
    return result


def fold_vert(partial_value):
    widened = with_halo(partial_value, (("vert", 1),), 2)
    interior = widened[:, 4:-4]
    interior = interior.at[:, :2].add(widened[:, :2])
    return interior.at[:, -2:].add(widened[:, -2:])


def fold_first(partial_value):
    widened = with_halo(partial_value, (("au", 2),), 2)
    interior = widened[:, :, 4:-4]
    interior = interior.at[:, :, :2].add(widened[:, :, :2])
    return interior.at[:, :, -2:].add(widened[:, :, -2:])


def shards(fields, coef_u, coef_v, coef_w, orient, link):
    highest = lax.Precision.HIGHEST
    stacked = fields[0]
    layers_w = stacked.shape[1]
    rows_v = stacked.shape[2]
    rows_u = stacked.shape[3]
    columns_v = rows_v // RATIO + 4
    columns_u = rows_u // RATIO + 4
    extended = with_halo(stacked, (("au", 3), ("vert", 2)), 3)
    density = field_density(extended, 3, 1, layers_w, rows_v, rows_u)
    inside_v = lax.axis_index("vert") * rows_v + jnp.arange(-1, rows_v + 1)
    inside_u = lax.axis_index("au") * rows_u + jnp.arange(-1, rows_u + 1)
    keep_v = (inside_v >= 0) & (inside_v < rows_v * lax.axis_size("vert"))
    keep_u = (inside_u >= 0) & (inside_u < rows_u * lax.axis_size("au"))
    keep = keep_v[:, None] & keep_u[None, :]
    smooth = blur(jnp.where(keep[None], density, 0.0))
    mat_v = band_matrix(coef_v, columns_v, 2)
    mat_u = band_matrix(coef_u, columns_u, 2)
    mat_w = band_matrix(coef_w, layers_w // RATIO, 0)
    reduced = jnp.einsum("wvu,wa->avu", smooth, mat_w, precision=highest)
    reduced = fold_vert(jnp.einsum("avu,vb->abu", reduced, mat_v, precision=highest))
    reduced = fold_first(jnp.einsum("abu,uc->abc", reduced, mat_u, precision=highest))
    patch_index = lax.axis_index("patch")
    patches = lax.axis_size("patch")
    layers_d = reduced.shape[0]
    out_index = jnp.where(orient[patch_index, 0] == 1, 0, layers_d - 1).astype(jnp.int32)
    in_index = jnp.where(orient[patch_index, 1] == 1, layers_d - 1, 0).astype(jnp.int32)
    layer_ids = jnp.arange(layers_d)
    out_mask = (layer_ids == out_index).astype(jnp.float32)[:, None, None]
    in_mask = (layer_ids == in_index).astype(jnp.float32)[:, None, None]
    out_face = jnp.sum(out_mask * reduced, axis=0)
    in_face = jnp.sum(in_mask * reduced, axis=0)
    gate_here = link[patch_index].astype(jnp.float32)
    gate_before = link[(patch_index + patches - 1) % patches].astype(jnp.float32)
    from_before = from_behind(out_face * gate_here, "patch", 1)
    from_after = from_behind(in_face * gate_before, "patch", -1)
    design = reduced + in_mask * from_before[None] + out_mask * from_after[None]
    return design[None]


def solution(mesh):
    placed = (P("patch", None, None, "vert", "au"), P(None, "au"), P(None, "vert"), P(), P(), P())
    return jax.shard_map(
        shards,
        mesh=mesh,
        in_specs=placed,
        out_specs=P("patch", None, "vert", "au"),
        check_vma=False,
    )
```

```python
import jax
import jax.numpy as jnp
from jax import lax
from jax.sharding import PartitionSpec as P

RATIO = 8


def with_halo(block, sides, width):
    for axis, dim in sides:
        count = lax.axis_size(axis)
        forward = [(i, i + 1) for i in range(count - 1)]
        backward = [(target, source) for source, target in forward]
        low = lax.ppermute(
            lax.slice_in_dim(block, block.shape[dim] - width, None, axis=dim), axis, forward
        )
        high = lax.ppermute(lax.slice_in_dim(block, 0, width, axis=dim), axis, backward)
        block = jnp.concatenate([low, block, high], axis=dim)
    return block


def from_behind(block, axis, distance):
    devices = range(lax.axis_size(axis))
    route = [((i - distance) % len(devices), i) for i in devices]
    return lax.ppermute(block, axis, route)


def field_density(extended, width, reach, layers_w, rows_v, rows_u):
    padded = jnp.pad(extended, ((0, 0), (2, 2), (0, 0), (0, 0)))
    channels = extended.shape[0]
    anchor = (0, 2, width - reach, width - reach)
    extent = (channels, layers_w, rows_v + 2 * reach, rows_u + 2 * reach)

    def shifted(direction, offset):
        corner_at = list(anchor)
        corner_at[direction] = corner_at[direction] + offset
        limit_at = tuple((b + s for b, s in zip(corner_at, extent)))
        return lax.slice(padded, tuple(corner_at), limit_at).astype(jnp.float32)

    centre = shifted(1, 0)
    product_sum = jnp.zeros(extent[1:], jnp.float32)
    div_flow = jnp.zeros(extent[1:], jnp.float32)
    div_adjoint = jnp.zeros(extent[1:], jnp.float32)
    for direction in (1, 2, 3):
        slopes = (
            8.0 * (shifted(direction, 1) - shifted(direction, -1))
            - (shifted(direction, 2) - shifted(direction, -2))
        ) / 12.0
        component = 3 - direction
        for k in range(3):
            product_sum = product_sum + slopes[k] * slopes[4 + k]
        div_flow = div_flow + slopes[component]
        div_adjoint = div_adjoint + slopes[4 + component]
    return product_sum - centre[3] * div_adjoint - centre[7] * div_flow


def blur(widened):
    padded = jnp.pad(widened, ((1, 1), (0, 0), (0, 0)))
    along_w = (padded[:-2] + 4.0 * padded[1:-1] + padded[2:]) / 6.0
    along_v = (along_w[:, :-2] + 4.0 * along_w[:, 1:-1] + along_w[:, 2:]) / 6.0
    return (along_v[:, :, :-2] + 4.0 * along_v[:, :, 1:-1] + along_v[:, :, 2:]) / 6.0


def band_matrix(coef_in, columns, offset):
    row_count = coef_in.shape[1]
    target = (jnp.arange(row_count) // RATIO)[:, None] + offset
    column = jnp.arange(columns)[None, :]
    result = jnp.zeros((row_count, columns), jnp.float32)
    for d in range(3):
        result = result + jnp.where(column == target + (d - 1), coef_in[d][:, None], 0.0)
    return result


def fold_vert(partial_value):
    widened = with_halo(partial_value, (("vert", 1),), 2)
    interior = widened[:, 4:-4]
    interior = interior.at[:, :2].add(widened[:, :2])
    return interior.at[:, -2:].add(widened[:, -2:])


def fold_first(partial_value):
    widened = with_halo(partial_value, (("au", 2),), 2)
    interior = widened[:, :, 4:-4]
    interior = interior.at[:, :, :2].add(widened[:, :, :2])
    return interior.at[:, :, -2:].add(widened[:, :, -2:])


def neighbour_rows(block, axis, dim, width):
    count = lax.axis_size(axis)
    forward = [(i, i + 1) for i in range(count - 1)]
    backward = [(target, source) for source, target in forward]
    low = lax.ppermute(
        lax.slice_in_dim(block, block.shape[dim] - width, None, axis=dim), axis, forward
    )
    high = lax.ppermute(lax.slice_in_dim(block, 0, width, axis=dim), axis, backward)
    return low, high


def slopes_along(low, core, high, dim):
    joined = jnp.concatenate([low, core, high], axis=dim)
    length = core.shape[dim]

    def shifted(offset):
        return lax.slice_in_dim(joined, 2 + offset, 2 + offset + length, axis=dim)

    return (8.0 * (shifted(1) - shifted(-1)) - (shifted(2) - shifted(-2))) / 12.0


def smoothed_band(coef_ext, columns, offset):
    rows = coef_ext.shape[1] - 2
    target = jnp.floor_divide(jnp.arange(-1, rows + 1), RATIO)[:, None] + offset
    column = jnp.arange(columns)[None, :]
    band = jnp.zeros((rows + 2, columns), jnp.float32)
    for d in range(3):
        band = band + jnp.where(column == target + (d - 1), coef_ext[d][:, None], 0.0)
    return (band[:-2] + 4.0 * band[1:-1] + band[2:]) / 6.0


def shards(fields, coef_u, coef_v, coef_w, orient, link):
    highest = lax.Precision.HIGHEST
    stacked = fields[0]
    layers_w = stacked.shape[1]
    rows_v = stacked.shape[2]
    rows_u = stacked.shape[3]
    columns_v = rows_v // RATIO + 4
    columns_u = rows_u // RATIO + 4
    moving = jnp.concatenate([stacked[0:3], stacked[4:7]], axis=0)
    low_u, high_u = neighbour_rows(moving, "au", 3, 2)
    low_v, high_v = neighbour_rows(moving, "vert", 2, 2)
    coef_low_u, coef_high_u = neighbour_rows(coef_u, "au", 1, 1)
    coef_low_v, coef_high_v = neighbour_rows(coef_v, "vert", 1, 1)
    values = stacked.astype(jnp.float32)
    moving = moving.astype(jnp.float32)
    zero_w = jnp.zeros_like(moving[:, :2])
    slopes = (
        slopes_along(zero_w, moving, zero_w, 1),
        slopes_along(low_v.astype(jnp.float32), moving, high_v.astype(jnp.float32), 2),
        slopes_along(low_u.astype(jnp.float32), moving, high_u.astype(jnp.float32), 3),
    )
    product_sum = jnp.zeros(values.shape[1:], jnp.float32)
    div_flow = jnp.zeros(values.shape[1:], jnp.float32)
    div_adjoint = jnp.zeros(values.shape[1:], jnp.float32)
    for direction, slope in enumerate(slopes):
        component = 2 - direction
        for k in range(3):
            product_sum = product_sum + slope[k] * slope[3 + k]
        div_flow = div_flow + slope[component]
        div_adjoint = div_adjoint + slope[3 + component]
    density = product_sum - values[3] * div_adjoint - values[7] * div_flow
    zero_coef = jnp.zeros_like(coef_w[:, :1])
    mat_w = smoothed_band(jnp.concatenate([zero_coef, coef_w, zero_coef], axis=1), layers_w // RATIO, 0)
    mat_v = smoothed_band(jnp.concatenate([coef_low_v, coef_v, coef_high_v], axis=1), columns_v, 2)
    mat_u = smoothed_band(jnp.concatenate([coef_low_u, coef_u, coef_high_u], axis=1), columns_u, 2)
    reduced = jnp.einsum("wvu,wa->avu", density, mat_w, precision=highest)
    reduced = fold_vert(jnp.einsum("avu,vb->abu", reduced, mat_v, precision=highest))
    reduced = fold_first(jnp.einsum("abu,uc->abc", reduced, mat_u, precision=highest))
    patch_index = lax.axis_index("patch")
    patches = lax.axis_size("patch")
    layers_d = reduced.shape[0]
    out_index = jnp.where(orient[patch_index, 0] == 1, 0, layers_d - 1).astype(jnp.int32)
    in_index = jnp.where(orient[patch_index, 1] == 1, layers_d - 1, 0).astype(jnp.int32)
    layer_ids = jnp.arange(layers_d)
    out_mask = (layer_ids == out_index).astype(jnp.float32)[:, None, None]
    in_mask = (layer_ids == in_index).astype(jnp.float32)[:, None, None]
    out_face = jnp.sum(out_mask * reduced, axis=0)
    in_face = jnp.sum(in_mask * reduced, axis=0)
    gate_here = link[patch_index].astype(jnp.float32)
    gate_before = link[(patch_index + patches - 1) % patches].astype(jnp.float32)
    from_before = from_behind(out_face * gate_here, "patch", 1)
    from_after = from_behind(in_face * gate_before, "patch", -1)
    design = reduced + in_mask * from_before[None] + out_mask * from_after[None]
    return design[None]


def solution(mesh):
    placed = (P("patch", None, None, "vert", "au"), P(None, "au"), P(None, "vert"), P(), P(), P())
    return jax.shard_map(
        shards,
        mesh=mesh,
        in_specs=placed,
        out_specs=P("patch", None, "vert", "au"),
        check_vma=False,
    )
```

```python
import jax
import jax.numpy as jnp
from jax import lax
from jax.sharding import PartitionSpec as P

RATIO = 8


def with_halo(block, sides, width):
    for axis, dim in sides:
        count = lax.axis_size(axis)
        forward = [(i, i + 1) for i in range(count - 1)]
        backward = [(target, source) for source, target in forward]
        low = lax.ppermute(
            lax.slice_in_dim(block, block.shape[dim] - width, None, axis=dim), axis, forward
        )
        high = lax.ppermute(lax.slice_in_dim(block, 0, width, axis=dim), axis, backward)
        block = jnp.concatenate([low, block, high], axis=dim)
    return block


def from_behind(block, axis, distance):
    devices = range(lax.axis_size(axis))
    route = [((i - distance) % len(devices), i) for i in devices]
    return lax.ppermute(block, axis, route)


def field_density(extended, width, reach, layers_w, rows_v, rows_u):
    padded = jnp.pad(extended, ((0, 0), (2, 2), (0, 0), (0, 0)))
    channels = extended.shape[0]
    anchor = (0, 2, width - reach, width - reach)
    extent = (channels, layers_w, rows_v + 2 * reach, rows_u + 2 * reach)

    def shifted(direction, offset):
        corner_at = list(anchor)
        corner_at[direction] = corner_at[direction] + offset
        limit_at = tuple((b + s for b, s in zip(corner_at, extent)))
        return lax.slice(padded, tuple(corner_at), limit_at).astype(jnp.float32)

    centre = shifted(1, 0)
    product_sum = jnp.zeros(extent[1:], jnp.float32)
    div_flow = jnp.zeros(extent[1:], jnp.float32)
    div_adjoint = jnp.zeros(extent[1:], jnp.float32)
    for direction in (1, 2, 3):
        slopes = (
            8.0 * (shifted(direction, 1) - shifted(direction, -1))
            - (shifted(direction, 2) - shifted(direction, -2))
        ) / 12.0
        component = 3 - direction
        for k in range(3):
            product_sum = product_sum + slopes[k] * slopes[4 + k]
        div_flow = div_flow + slopes[component]
        div_adjoint = div_adjoint + slopes[4 + component]
    return product_sum - centre[3] * div_adjoint - centre[7] * div_flow


def blur(widened):
    padded = jnp.pad(widened, ((1, 1), (0, 0), (0, 0)))
    along_w = (padded[:-2] + 4.0 * padded[1:-1] + padded[2:]) / 6.0
    along_v = (along_w[:, :-2] + 4.0 * along_w[:, 1:-1] + along_w[:, 2:]) / 6.0
    return (along_v[:, :, :-2] + 4.0 * along_v[:, :, 1:-1] + along_v[:, :, 2:]) / 6.0


def band_matrix(coef_in, columns, offset):
    row_count = coef_in.shape[1]
    target = (jnp.arange(row_count) // RATIO)[:, None] + offset
    column = jnp.arange(columns)[None, :]
    result = jnp.zeros((row_count, columns), jnp.float32)
    for d in range(3):
        result = result + jnp.where(column == target + (d - 1), coef_in[d][:, None], 0.0)
    return result


def fold_vert(partial_value):
    widened = with_halo(partial_value, (("vert", 1),), 2)
    interior = widened[:, 4:-4]
    interior = interior.at[:, :2].add(widened[:, :2])
    return interior.at[:, -2:].add(widened[:, -2:])


def fold_first(partial_value):
    widened = with_halo(partial_value, (("au", 2),), 2)
    interior = widened[:, :, 4:-4]
    interior = interior.at[:, :, :2].add(widened[:, :, :2])
    return interior.at[:, :, -2:].add(widened[:, :, -2:])


def split_exact(vector):
    high = lax.reduce_precision(vector, exponent_bits=8, mantissa_bits=7)
    rest = vector - high
    middle = lax.reduce_precision(rest, exponent_bits=8, mantissa_bits=7)
    low = rest - middle
    return jnp.stack([high, middle, low]).astype(jnp.bfloat16).reshape(-1)


def join_exact(parts):
    high, middle, low = parts.astype(jnp.float32).reshape(3, -1)
    return high + (middle + low)


def with_rider(piece, vector):
    parts = split_exact(vector)
    carried = piece.shape[1]
    assert parts.shape[0] <= carried
    parts = jnp.pad(parts, (0, carried - parts.shape[0]))
    shape = (1,) + piece.shape[1:]
    slab = jnp.broadcast_to(parts.reshape((1, carried) + (1,) * (piece.ndim - 2)), shape)
    return jnp.concatenate([piece, slab], axis=0)


def neighbour_rows(block, coef, axis, dim, width):
    count = lax.axis_size(axis)
    forward = [(i, i + 1) for i in range(count - 1)]
    backward = [(target, source) for source, target in forward]
    size = coef.shape[0] * 3
    low = lax.ppermute(
        with_rider(lax.slice_in_dim(block, block.shape[dim] - width, None, axis=dim), coef[:, -1]),
        axis,
        forward,
    )
    high = lax.ppermute(with_rider(lax.slice_in_dim(block, 0, width, axis=dim), coef[:, 0]), axis, backward)
    rider_at = (-1, slice(0, size)) + (0,) * (block.ndim - 2)
    coef_low = join_exact(low[rider_at])[:, None]
    coef_high = join_exact(high[rider_at])[:, None]
    return low[:-1], high[:-1], coef_low, coef_high


def slopes_along(low, core, high, dim):
    joined = jnp.concatenate([low, core, high], axis=dim)
    length = core.shape[dim]

    def shifted(offset):
        return lax.slice_in_dim(joined, 2 + offset, 2 + offset + length, axis=dim)

    return (8.0 * (shifted(1) - shifted(-1)) - (shifted(2) - shifted(-2))) / 12.0


def smoothed_band(coef_ext, columns, offset):
    rows = coef_ext.shape[1] - 2
    target = jnp.floor_divide(jnp.arange(-1, rows + 1), RATIO)[:, None] + offset
    column = jnp.arange(columns)[None, :]
    band = jnp.zeros((rows + 2, columns), jnp.float32)
    for d in range(3):
        band = band + jnp.where(column == target + (d - 1), coef_ext[d][:, None], 0.0)
    return (band[:-2] + 4.0 * band[1:-1] + band[2:]) / 6.0


def shards(fields, coef_u, coef_v, coef_w, orient, link):
    highest = lax.Precision.HIGHEST
    stacked = fields[0]
    layers_w = stacked.shape[1]
    rows_v = stacked.shape[2]
    rows_u = stacked.shape[3]
    columns_v = rows_v // RATIO + 4
    columns_u = rows_u // RATIO + 4
    moving = jnp.concatenate([stacked[0:3], stacked[4:7]], axis=0)
    low_u, high_u, coef_low_u, coef_high_u = neighbour_rows(moving, coef_u, "au", 3, 2)
    low_v, high_v, coef_low_v, coef_high_v = neighbour_rows(moving, coef_v, "vert", 2, 2)
    values = stacked.astype(jnp.float32)
    moving = moving.astype(jnp.float32)
    zero_w = jnp.zeros_like(moving[:, :2])
    slopes = (
        slopes_along(zero_w, moving, zero_w, 1),
        slopes_along(low_v.astype(jnp.float32), moving, high_v.astype(jnp.float32), 2),
        slopes_along(low_u.astype(jnp.float32), moving, high_u.astype(jnp.float32), 3),
    )
    product_sum = jnp.zeros(values.shape[1:], jnp.float32)
    div_flow = jnp.zeros(values.shape[1:], jnp.float32)
    div_adjoint = jnp.zeros(values.shape[1:], jnp.float32)
    for direction, slope in enumerate(slopes):
        component = 2 - direction
        for k in range(3):
            product_sum = product_sum + slope[k] * slope[3 + k]
        div_flow = div_flow + slope[component]
        div_adjoint = div_adjoint + slope[3 + component]
    density = product_sum - values[3] * div_adjoint - values[7] * div_flow
    zero_coef = jnp.zeros_like(coef_w[:, :1])
    mat_w = smoothed_band(jnp.concatenate([zero_coef, coef_w, zero_coef], axis=1), layers_w // RATIO, 0)
    mat_v = smoothed_band(jnp.concatenate([coef_low_v, coef_v, coef_high_v], axis=1), columns_v, 2)
    mat_u = smoothed_band(jnp.concatenate([coef_low_u, coef_u, coef_high_u], axis=1), columns_u, 2)
    reduced = jnp.einsum("wvu,wa->avu", density, mat_w, precision=highest)
    reduced = fold_vert(jnp.einsum("avu,vb->abu", reduced, mat_v, precision=highest))
    reduced = fold_first(jnp.einsum("abu,uc->abc", reduced, mat_u, precision=highest))
    patch_index = lax.axis_index("patch")
    patches = lax.axis_size("patch")
    layers_d = reduced.shape[0]
    out_index = jnp.where(orient[patch_index, 0] == 1, 0, layers_d - 1).astype(jnp.int32)
    in_index = jnp.where(orient[patch_index, 1] == 1, layers_d - 1, 0).astype(jnp.int32)
    layer_ids = jnp.arange(layers_d)
    out_mask = (layer_ids == out_index).astype(jnp.float32)[:, None, None]
    in_mask = (layer_ids == in_index).astype(jnp.float32)[:, None, None]
    out_face = jnp.sum(out_mask * reduced, axis=0)
    in_face = jnp.sum(in_mask * reduced, axis=0)
    gate_here = link[patch_index].astype(jnp.float32)
    gate_before = link[(patch_index + patches - 1) % patches].astype(jnp.float32)
    from_before = from_behind(out_face * gate_here, "patch", 1)
    from_after = from_behind(in_face * gate_before, "patch", -1)
    design = reduced + in_mask * from_before[None] + out_mask * from_after[None]
    return design[None]


def solution(mesh):
    placed = (P("patch", None, None, "vert", "au"), P(None, "au"), P(None, "vert"), P(), P(), P())
    return jax.shard_map(
        shards,
        mesh=mesh,
        in_specs=placed,
        out_specs=P("patch", None, "vert", "au"),
        check_vma=False,
    )
```

```python
import jax
import jax.numpy as jnp
from jax import lax
from jax.sharding import PartitionSpec as P

RATIO = 8


def with_halo(block, sides, width):
    for axis, dim in sides:
        count = lax.axis_size(axis)
        forward = [(i, i + 1) for i in range(count - 1)]
        backward = [(target, source) for source, target in forward]
        low = lax.ppermute(
            lax.slice_in_dim(block, block.shape[dim] - width, None, axis=dim), axis, forward
        )
        high = lax.ppermute(lax.slice_in_dim(block, 0, width, axis=dim), axis, backward)
        block = jnp.concatenate([low, block, high], axis=dim)
    return block


def from_behind(block, axis, distance):
    devices = range(lax.axis_size(axis))
    route = [((i - distance) % len(devices), i) for i in devices]
    return lax.ppermute(block, axis, route)


def field_density(extended, width, reach, layers_w, rows_v, rows_u):
    padded = jnp.pad(extended, ((0, 0), (2, 2), (0, 0), (0, 0)))
    channels = extended.shape[0]
    anchor = (0, 2, width - reach, width - reach)
    extent = (channels, layers_w, rows_v + 2 * reach, rows_u + 2 * reach)

    def shifted(direction, offset):
        corner_at = list(anchor)
        corner_at[direction] = corner_at[direction] + offset
        limit_at = tuple((b + s for b, s in zip(corner_at, extent)))
        return lax.slice(padded, tuple(corner_at), limit_at).astype(jnp.float32)

    centre = shifted(1, 0)
    product_sum = jnp.zeros(extent[1:], jnp.float32)
    div_flow = jnp.zeros(extent[1:], jnp.float32)
    div_adjoint = jnp.zeros(extent[1:], jnp.float32)
    for direction in (1, 2, 3):
        slopes = (
            8.0 * (shifted(direction, 1) - shifted(direction, -1))
            - (shifted(direction, 2) - shifted(direction, -2))
        ) / 12.0
        component = 3 - direction
        for k in range(3):
            product_sum = product_sum + slopes[k] * slopes[4 + k]
        div_flow = div_flow + slopes[component]
        div_adjoint = div_adjoint + slopes[4 + component]
    return product_sum - centre[3] * div_adjoint - centre[7] * div_flow


def blur(widened):
    padded = jnp.pad(widened, ((1, 1), (0, 0), (0, 0)))
    along_w = (padded[:-2] + 4.0 * padded[1:-1] + padded[2:]) / 6.0
    along_v = (along_w[:, :-2] + 4.0 * along_w[:, 1:-1] + along_w[:, 2:]) / 6.0
    return (along_v[:, :, :-2] + 4.0 * along_v[:, :, 1:-1] + along_v[:, :, 2:]) / 6.0


def band_matrix(coef_in, columns, offset):
    row_count = coef_in.shape[1]
    target = (jnp.arange(row_count) // RATIO)[:, None] + offset
    column = jnp.arange(columns)[None, :]
    result = jnp.zeros((row_count, columns), jnp.float32)
    for d in range(3):
        result = result + jnp.where(column == target + (d - 1), coef_in[d][:, None], 0.0)
    return result


def fold_both(partial_value, spill):
    count_u = lax.axis_size("au")
    count_v = lax.axis_size("vert")
    rows = partial_value.shape[1] - 2 * spill
    cols = partial_value.shape[2] - 2 * spill
    assert rows >= spill and cols >= spill

    def send(piece, step_u, step_v):
        route = []
        for a in range(count_u):
            for v in range(count_v):
                if 0 <= a + step_u < count_u and 0 <= v + step_v < count_v:
                    route.append((a * count_v + v, (a + step_u) * count_v + v + step_v))
        return lax.ppermute(piece, ("au", "vert"), route)

    inner_v = slice(spill, spill + rows)
    inner_u = slice(spill, spill + cols)
    low_v = slice(0, spill)
    high_v = slice(spill + rows, None)
    low_u = slice(0, spill)
    high_u = slice(spill + cols, None)
    design = partial_value[:, inner_v, inner_u]
    from_v_low = send(partial_value[:, high_v, inner_u], 0, 1)
    from_v_high = send(partial_value[:, low_v, inner_u], 0, -1)
    from_u_low = send(partial_value[:, inner_v, high_u], 1, 0)
    from_u_high = send(partial_value[:, inner_v, low_u], -1, 0)
    from_corner_ll = send(partial_value[:, high_v, high_u], 1, 1)
    from_corner_lh = send(partial_value[:, low_v, high_u], 1, -1)
    from_corner_hl = send(partial_value[:, high_v, low_u], -1, 1)
    from_corner_hh = send(partial_value[:, low_v, low_u], -1, -1)
    design = design.at[:, :spill, :].add(from_v_low)
    design = design.at[:, rows - spill:, :].add(from_v_high)
    design = design.at[:, :, :spill].add(from_u_low)
    design = design.at[:, :, cols - spill:].add(from_u_high)
    design = design.at[:, :spill, :spill].add(from_corner_ll)
    design = design.at[:, rows - spill:, :spill].add(from_corner_lh)
    design = design.at[:, :spill, cols - spill:].add(from_corner_hl)
    design = design.at[:, rows - spill:, cols - spill:].add(from_corner_hh)
    return design


def split_exact(vector):
    high = lax.reduce_precision(vector, exponent_bits=8, mantissa_bits=7)
    rest = vector - high
    middle = lax.reduce_precision(rest, exponent_bits=8, mantissa_bits=7)
    low = rest - middle
    return jnp.stack([high, middle, low]).astype(jnp.bfloat16).reshape(-1)


def join_exact(parts):
    high, middle, low = parts.astype(jnp.float32).reshape(3, -1)
    return high + (middle + low)


def with_rider(piece, vector):
    parts = split_exact(vector)
    carried = piece.shape[1]
    assert parts.shape[0] <= carried
    parts = jnp.pad(parts, (0, carried - parts.shape[0]))
    shape = (1,) + piece.shape[1:]
    slab = jnp.broadcast_to(parts.reshape((1, carried) + (1,) * (piece.ndim - 2)), shape)
    return jnp.concatenate([piece, slab], axis=0)


def neighbour_rows(block, coef, axis, dim, width):
    count = lax.axis_size(axis)
    forward = [(i, i + 1) for i in range(count - 1)]
    backward = [(target, source) for source, target in forward]
    size = coef.shape[0] * 3
    low = lax.ppermute(
        with_rider(lax.slice_in_dim(block, block.shape[dim] - width, None, axis=dim), coef[:, -1]),
        axis,
        forward,
    )
    high = lax.ppermute(with_rider(lax.slice_in_dim(block, 0, width, axis=dim), coef[:, 0]), axis, backward)
    rider_at = (-1, slice(0, size)) + (0,) * (block.ndim - 2)
    coef_low = join_exact(low[rider_at])[:, None]
    coef_high = join_exact(high[rider_at])[:, None]
    return low[:-1], high[:-1], coef_low, coef_high


def slopes_along(low, core, high, dim):
    joined = jnp.concatenate([low, core, high], axis=dim)
    length = core.shape[dim]

    def shifted(offset):
        return lax.slice_in_dim(joined, 2 + offset, 2 + offset + length, axis=dim)

    return (8.0 * (shifted(1) - shifted(-1)) - (shifted(2) - shifted(-2))) / 12.0


def smoothed_band(coef_ext, columns, offset):
    rows = coef_ext.shape[1] - 2
    target = jnp.floor_divide(jnp.arange(-1, rows + 1), RATIO)[:, None] + offset
    column = jnp.arange(columns)[None, :]
    band = jnp.zeros((rows + 2, columns), jnp.float32)
    for d in range(3):
        band = band + jnp.where(column == target + (d - 1), coef_ext[d][:, None], 0.0)
    return (band[:-2] + 4.0 * band[1:-1] + band[2:]) / 6.0


def shards(fields, coef_u, coef_v, coef_w, orient, link):
    highest = lax.Precision.HIGHEST
    stacked = fields[0]
    layers_w = stacked.shape[1]
    rows_v = stacked.shape[2]
    rows_u = stacked.shape[3]
    columns_v = rows_v // RATIO + 4
    columns_u = rows_u // RATIO + 4
    moving = jnp.concatenate([stacked[0:3], stacked[4:7]], axis=0)
    low_u, high_u, coef_low_u, coef_high_u = neighbour_rows(moving, coef_u, "au", 3, 2)
    low_v, high_v, coef_low_v, coef_high_v = neighbour_rows(moving, coef_v, "vert", 2, 2)
    values = stacked.astype(jnp.float32)
    moving = moving.astype(jnp.float32)
    zero_w = jnp.zeros_like(moving[:, :2])
    slopes = (
        slopes_along(zero_w, moving, zero_w, 1),
        slopes_along(low_v.astype(jnp.float32), moving, high_v.astype(jnp.float32), 2),
        slopes_along(low_u.astype(jnp.float32), moving, high_u.astype(jnp.float32), 3),
    )
    product_sum = jnp.zeros(values.shape[1:], jnp.float32)
    div_flow = jnp.zeros(values.shape[1:], jnp.float32)
    div_adjoint = jnp.zeros(values.shape[1:], jnp.float32)
    for direction, slope in enumerate(slopes):
        component = 2 - direction
        for k in range(3):
            product_sum = product_sum + slope[k] * slope[3 + k]
        div_flow = div_flow + slope[component]
        div_adjoint = div_adjoint + slope[3 + component]
    density = product_sum - values[3] * div_adjoint - values[7] * div_flow
    zero_coef = jnp.zeros_like(coef_w[:, :1])
    mat_w = smoothed_band(jnp.concatenate([zero_coef, coef_w, zero_coef], axis=1), layers_w // RATIO, 0)
    mat_v = smoothed_band(jnp.concatenate([coef_low_v, coef_v, coef_high_v], axis=1), columns_v, 2)
    mat_u = smoothed_band(jnp.concatenate([coef_low_u, coef_u, coef_high_u], axis=1), columns_u, 2)
    reduced = jnp.einsum("wvu,wa->avu", density, mat_w, precision=highest)
    reduced = jnp.einsum("avu,vb->abu", reduced, mat_v, precision=highest)
    reduced = fold_both(jnp.einsum("abu,uc->abc", reduced, mat_u, precision=highest), 2)
    patch_index = lax.axis_index("patch")
    patches = lax.axis_size("patch")
    layers_d = reduced.shape[0]
    out_index = jnp.where(orient[patch_index, 0] == 1, 0, layers_d - 1).astype(jnp.int32)
    in_index = jnp.where(orient[patch_index, 1] == 1, layers_d - 1, 0).astype(jnp.int32)
    layer_ids = jnp.arange(layers_d)
    out_mask = (layer_ids == out_index).astype(jnp.float32)[:, None, None]
    in_mask = (layer_ids == in_index).astype(jnp.float32)[:, None, None]
    out_face = jnp.sum(out_mask * reduced, axis=0)
    in_face = jnp.sum(in_mask * reduced, axis=0)
    gate_here = link[patch_index].astype(jnp.float32)
    gate_before = link[(patch_index + patches - 1) % patches].astype(jnp.float32)
    from_before = from_behind(out_face * gate_here, "patch", 1)
    from_after = from_behind(in_face * gate_before, "patch", -1)
    design = reduced + in_mask * from_before[None] + out_mask * from_after[None]
    return design[None]


def solution(mesh):
    placed = (P("patch", None, None, "vert", "au"), P(None, "au"), P(None, "vert"), P(), P(), P())
    return jax.shard_map(
        shards,
        mesh=mesh,
        in_specs=placed,
        out_specs=P("patch", None, "vert", "au"),
        check_vma=False,
    )
```

```python
import jax
import jax.numpy as jnp
from jax import lax
from jax.sharding import PartitionSpec as P

RATIO = 8


def with_halo(block, sides, width):
    for axis, dim in sides:
        count = lax.axis_size(axis)
        forward = [(i, i + 1) for i in range(count - 1)]
        backward = [(target, source) for source, target in forward]
        low = lax.ppermute(
            lax.slice_in_dim(block, block.shape[dim] - width, None, axis=dim), axis, forward
        )
        high = lax.ppermute(lax.slice_in_dim(block, 0, width, axis=dim), axis, backward)
        block = jnp.concatenate([low, block, high], axis=dim)
    return block


def from_behind(block, axis, distance):
    devices = range(lax.axis_size(axis))
    route = [((i - distance) % len(devices), i) for i in devices]
    return lax.ppermute(block, axis, route)


def field_density(extended, width, reach, layers_w, rows_v, rows_u):
    padded = jnp.pad(extended, ((0, 0), (2, 2), (0, 0), (0, 0)))
    channels = extended.shape[0]
    anchor = (0, 2, width - reach, width - reach)
    extent = (channels, layers_w, rows_v + 2 * reach, rows_u + 2 * reach)

    def shifted(direction, offset):
        corner_at = list(anchor)
        corner_at[direction] = corner_at[direction] + offset
        limit_at = tuple((b + s for b, s in zip(corner_at, extent)))
        return lax.slice(padded, tuple(corner_at), limit_at).astype(jnp.float32)

    centre = shifted(1, 0)
    product_sum = jnp.zeros(extent[1:], jnp.float32)
    div_flow = jnp.zeros(extent[1:], jnp.float32)
    div_adjoint = jnp.zeros(extent[1:], jnp.float32)
    for direction in (1, 2, 3):
        slopes = (
            8.0 * (shifted(direction, 1) - shifted(direction, -1))
            - (shifted(direction, 2) - shifted(direction, -2))
        ) / 12.0
        component = 3 - direction
        for k in range(3):
            product_sum = product_sum + slopes[k] * slopes[4 + k]
        div_flow = div_flow + slopes[component]
        div_adjoint = div_adjoint + slopes[4 + component]
    return product_sum - centre[3] * div_adjoint - centre[7] * div_flow


def blur(widened):
    padded = jnp.pad(widened, ((1, 1), (0, 0), (0, 0)))
    along_w = (padded[:-2] + 4.0 * padded[1:-1] + padded[2:]) / 6.0
    along_v = (along_w[:, :-2] + 4.0 * along_w[:, 1:-1] + along_w[:, 2:]) / 6.0
    return (along_v[:, :, :-2] + 4.0 * along_v[:, :, 1:-1] + along_v[:, :, 2:]) / 6.0


def band_matrix(coef_in, columns, offset):
    row_count = coef_in.shape[1]
    target = (jnp.arange(row_count) // RATIO)[:, None] + offset
    column = jnp.arange(columns)[None, :]
    result = jnp.zeros((row_count, columns), jnp.float32)
    for d in range(3):
        result = result + jnp.where(column == target + (d - 1), coef_in[d][:, None], 0.0)
    return result


def fold_vert(partial_value):
    widened = with_halo(partial_value, (("vert", 1),), 2)
    interior = widened[:, 4:-4]
    interior = interior.at[:, :2].add(widened[:, :2])
    return interior.at[:, -2:].add(widened[:, -2:])


def fold_first(partial_value):
    widened = with_halo(partial_value, (("au", 2),), 2)
    interior = widened[:, :, 4:-4]
    interior = interior.at[:, :, :2].add(widened[:, :, :2])
    return interior.at[:, :, -2:].add(widened[:, :, -2:])


def split_exact(vector):
    high = lax.reduce_precision(vector, exponent_bits=8, mantissa_bits=7)
    rest = vector - high
    middle = lax.reduce_precision(rest, exponent_bits=8, mantissa_bits=7)
    low = rest - middle
    return jnp.stack([high, middle, low]).astype(jnp.bfloat16).reshape(-1)


def join_exact(parts):
    high, middle, low = parts.astype(jnp.float32).reshape(3, -1)
    return high + (middle + low)


def rider_dim(piece):
    return piece.ndim - 1 if piece.shape[-1] >= 9 else piece.ndim - 2


def with_rider(piece, vector):
    parts = split_exact(vector)
    dim = rider_dim(piece)
    carried = piece.shape[dim]
    assert parts.shape[0] <= carried
    parts = jnp.pad(parts, (0, carried - parts.shape[0]))
    shape = (1,) + piece.shape[1:]
    layout = [1] * piece.ndim
    layout[dim] = carried
    slab = jnp.broadcast_to(parts.reshape(layout), shape)
    return jnp.concatenate([piece, slab], axis=0)


def neighbour_rows(block, coef, axis, dim, width):
    count = lax.axis_size(axis)
    forward = [(i, i + 1) for i in range(count - 1)]
    backward = [(target, source) for source, target in forward]
    size = coef.shape[0] * 3
    low = lax.ppermute(
        with_rider(lax.slice_in_dim(block, block.shape[dim] - width, None, axis=dim), coef[:, -1]),
        axis,
        forward,
    )
    high = lax.ppermute(with_rider(lax.slice_in_dim(block, 0, width, axis=dim), coef[:, 0]), axis, backward)
    rider_at = [-1] + [0] * (block.ndim - 1)
    rider_at[rider_dim(low)] = slice(0, size)
    rider_at = tuple(rider_at)
    coef_low = join_exact(low[rider_at])[:, None]
    coef_high = join_exact(high[rider_at])[:, None]
    return low[:-1], high[:-1], coef_low, coef_high


def slopes_along(low, core, high, dim):
    joined = jnp.concatenate([low, core, high], axis=dim)
    length = core.shape[dim]

    def shifted(offset):
        return lax.slice_in_dim(joined, 2 + offset, 2 + offset + length, axis=dim).astype(jnp.float32)

    return (8.0 * (shifted(1) - shifted(-1)) - (shifted(2) - shifted(-2))) / 12.0


def smoothed_band(coef_ext, columns, offset):
    rows = coef_ext.shape[1] - 2
    target = jnp.floor_divide(jnp.arange(-1, rows + 1), RATIO)[:, None] + offset
    column = jnp.arange(columns)[None, :]
    band = jnp.zeros((rows + 2, columns), jnp.float32)
    for d in range(3):
        band = band + jnp.where(column == target + (d - 1), coef_ext[d][:, None], 0.0)
    return (band[:-2] + 4.0 * band[1:-1] + band[2:]) / 6.0


def shards(fields, coef_u, coef_v, coef_w, orient, link):
    highest = lax.Precision.HIGHEST
    stacked = fields[0]
    layers_w = stacked.shape[1]
    rows_v = stacked.shape[2]
    rows_u = stacked.shape[3]
    columns_v = rows_v // RATIO + 4
    columns_u = rows_u // RATIO + 4
    moving = jnp.concatenate([stacked[0:3], stacked[4:7]], axis=0)
    low_u, high_u, coef_low_u, coef_high_u = neighbour_rows(moving, coef_u, "au", 3, 2)
    low_v, high_v, coef_low_v, coef_high_v = neighbour_rows(moving, coef_v, "vert", 2, 2)
    values = stacked.astype(jnp.float32)
    zero_w = jnp.zeros_like(moving[:, :2])
    slopes = (
        slopes_along(zero_w, moving, zero_w, 1),
        slopes_along(low_v, moving, high_v, 2),
        slopes_along(low_u, moving, high_u, 3),
    )
    product_sum = jnp.zeros(values.shape[1:], jnp.float32)
    div_flow = jnp.zeros(values.shape[1:], jnp.float32)
    div_adjoint = jnp.zeros(values.shape[1:], jnp.float32)
    for direction, slope in enumerate(slopes):
        component = 2 - direction
        for k in range(3):
            product_sum = product_sum + slope[k] * slope[3 + k]
        div_flow = div_flow + slope[component]
        div_adjoint = div_adjoint + slope[3 + component]
    density = product_sum - values[3] * div_adjoint - values[7] * div_flow
    zero_coef = jnp.zeros_like(coef_w[:, :1])
    mat_w = smoothed_band(jnp.concatenate([zero_coef, coef_w, zero_coef], axis=1), layers_w // RATIO, 0)
    mat_v = smoothed_band(jnp.concatenate([coef_low_v, coef_v, coef_high_v], axis=1), columns_v, 2)
    mat_u = smoothed_band(jnp.concatenate([coef_low_u, coef_u, coef_high_u], axis=1), columns_u, 2)
    reduced = jnp.einsum("wvu,wa->avu", density, mat_w, precision=highest)
    reduced = fold_vert(jnp.einsum("avu,vb->abu", reduced, mat_v, precision=highest))
    reduced = fold_first(jnp.einsum("abu,uc->abc", reduced, mat_u, precision=highest))
    patch_index = lax.axis_index("patch")
    patches = lax.axis_size("patch")
    layers_d = reduced.shape[0]
    out_index = jnp.where(orient[patch_index, 0] == 1, 0, layers_d - 1).astype(jnp.int32)
    in_index = jnp.where(orient[patch_index, 1] == 1, layers_d - 1, 0).astype(jnp.int32)
    layer_ids = jnp.arange(layers_d)
    out_mask = (layer_ids == out_index).astype(jnp.float32)[:, None, None]
    in_mask = (layer_ids == in_index).astype(jnp.float32)[:, None, None]
    out_face = jnp.sum(out_mask * reduced, axis=0)
    in_face = jnp.sum(in_mask * reduced, axis=0)
    gate_here = link[patch_index].astype(jnp.float32)
    gate_before = link[(patch_index + patches - 1) % patches].astype(jnp.float32)
    from_before = from_behind(out_face * gate_here, "patch", 1)
    from_after = from_behind(in_face * gate_before, "patch", -1)
    design = reduced + in_mask * from_before[None] + out_mask * from_after[None]
    return design[None]


def solution(mesh):
    placed = (P("patch", None, None, "vert", "au"), P(None, "au"), P(None, "vert"), P(), P(), P())
    return jax.shard_map(
        shards,
        mesh=mesh,
        in_specs=placed,
        out_specs=P("patch", None, "vert", "au"),
        check_vma=False,
    )
```

```python
import numpy as np
import jax
import jax.numpy as jnp
from jax import lax
from jax.sharding import PartitionSpec as P

RATIO = 8


def with_halo(block, sides, width):
    for axis, dim in sides:
        count = lax.axis_size(axis)
        forward = [(i, i + 1) for i in range(count - 1)]
        backward = [(target, source) for source, target in forward]
        low = lax.ppermute(
            lax.slice_in_dim(block, block.shape[dim] - width, None, axis=dim), axis, forward
        )
        high = lax.ppermute(lax.slice_in_dim(block, 0, width, axis=dim), axis, backward)
        block = jnp.concatenate([low, block, high], axis=dim)
    return block


def from_behind(block, axis, distance):
    devices = range(lax.axis_size(axis))
    route = [((i - distance) % len(devices), i) for i in devices]
    return lax.ppermute(block, axis, route)


def field_density(extended, width, reach, layers_w, rows_v, rows_u):
    padded = jnp.pad(extended, ((0, 0), (2, 2), (0, 0), (0, 0)))
    channels = extended.shape[0]
    anchor = (0, 2, width - reach, width - reach)
    extent = (channels, layers_w, rows_v + 2 * reach, rows_u + 2 * reach)

    def shifted(direction, offset):
        corner_at = list(anchor)
        corner_at[direction] = corner_at[direction] + offset
        limit_at = tuple((b + s for b, s in zip(corner_at, extent)))
        return lax.slice(padded, tuple(corner_at), limit_at).astype(jnp.float32)

    centre = shifted(1, 0)
    product_sum = jnp.zeros(extent[1:], jnp.float32)
    div_flow = jnp.zeros(extent[1:], jnp.float32)
    div_adjoint = jnp.zeros(extent[1:], jnp.float32)
    for direction in (1, 2, 3):
        slopes = (
            8.0 * (shifted(direction, 1) - shifted(direction, -1))
            - (shifted(direction, 2) - shifted(direction, -2))
        ) / 12.0
        component = 3 - direction
        for k in range(3):
            product_sum = product_sum + slopes[k] * slopes[4 + k]
        div_flow = div_flow + slopes[component]
        div_adjoint = div_adjoint + slopes[4 + component]
    return product_sum - centre[3] * div_adjoint - centre[7] * div_flow


def blur(widened):
    padded = jnp.pad(widened, ((1, 1), (0, 0), (0, 0)))
    along_w = (padded[:-2] + 4.0 * padded[1:-1] + padded[2:]) / 6.0
    along_v = (along_w[:, :-2] + 4.0 * along_w[:, 1:-1] + along_w[:, 2:]) / 6.0
    return (along_v[:, :, :-2] + 4.0 * along_v[:, :, 1:-1] + along_v[:, :, 2:]) / 6.0


def band_matrix(coef_in, columns, offset):
    row_count = coef_in.shape[1]
    target = (jnp.arange(row_count) // RATIO)[:, None] + offset
    column = jnp.arange(columns)[None, :]
    result = jnp.zeros((row_count, columns), jnp.float32)
    for d in range(3):
        result = result + jnp.where(column == target + (d - 1), coef_in[d][:, None], 0.0)
    return result


def fold_vert(partial_value):
    widened = with_halo(partial_value, (("vert", 1),), 2)
    interior = widened[:, 4:-4]
    interior = interior.at[:, :2].add(widened[:, :2])
    return interior.at[:, -2:].add(widened[:, -2:])


def fold_first(partial_value):
    widened = with_halo(partial_value, (("au", 2),), 2)
    interior = widened[:, :, 4:-4]
    interior = interior.at[:, :, :2].add(widened[:, :, :2])
    return interior.at[:, :, -2:].add(widened[:, :, -2:])


def split_exact(vector):
    high = lax.reduce_precision(vector, exponent_bits=8, mantissa_bits=7)
    rest = vector - high
    middle = lax.reduce_precision(rest, exponent_bits=8, mantissa_bits=7)
    low = rest - middle
    return jnp.stack([high, middle, low]).astype(jnp.bfloat16)


def join_exact(parts):
    parts = parts.astype(jnp.float32)
    return parts[0] + (parts[1] + parts[2])


def spread_dim(piece):
    return piece.ndim - 1 if piece.shape[-1] >= 3 else piece.ndim - 2


def with_rider(piece, vector):
    parts = split_exact(vector)
    shape = (1,) + piece.shape[1:]
    spread = spread_dim(piece)
    assert shape[1] >= parts.shape[0] and shape[spread] >= parts.shape[1]
    grid = jnp.pad(parts, ((0, shape[1] - parts.shape[0]), (0, shape[spread] - parts.shape[1])))
    layout = [1] * piece.ndim
    layout[1] = shape[1]
    layout[spread] = shape[spread]
    slab = jnp.broadcast_to(grid.reshape(layout), shape)
    return jnp.concatenate([piece, slab], axis=0)


def neighbour_rows(stacked, coef, axis, dim, width):
    count = lax.axis_size(axis)
    forward = [(i, i + 1) for i in range(count - 1)]
    backward = [(target, source) for source, target in forward]
    length = stacked.shape[dim]
    low = lax.ppermute(
        with_rider(lax.slice_in_dim(stacked, length - width, None, axis=dim), coef[:, -1]), axis, forward
    )
    high = lax.ppermute(with_rider(lax.slice_in_dim(stacked, 0, width, axis=dim), coef[:, 0]), axis, backward)
    rider_at = [-1, slice(0, 3)] + [0] * (stacked.ndim - 2)
    rider_at[spread_dim(low)] = slice(0, coef.shape[0])
    rider_at = tuple(rider_at)
    coef_low = join_exact(low[rider_at])[:, None]
    coef_high = join_exact(high[rider_at])[:, None]
    return low[:-1], high[:-1], coef_low, coef_high


def slopes_along(low, core, high, dim):
    joined = jnp.concatenate([low.astype(jnp.float32), core, high.astype(jnp.float32)], axis=dim)
    length = core.shape[dim]

    def shifted(offset):
        return lax.slice_in_dim(joined, 2 + offset, 2 + offset + length, axis=dim)

    return (8.0 * (shifted(1) - shifted(-1)) - (shifted(2) - shifted(-2))) / 12.0


def smoothed_band(coef_ext, columns, offset):
    rows = coef_ext.shape[1] - 2
    target = np.floor_divide(np.arange(-1, rows + 1), RATIO)[:, None] + offset
    column = np.arange(columns)[None, :]
    band = jnp.zeros((rows + 2, columns), jnp.float32)
    for d in range(3):
        band = band + jnp.where(column == target + (d - 1), coef_ext[d][:, None], 0.0)
    return (band[:-2] + 4.0 * band[1:-1] + band[2:]) / 6.0


def shards(fields, coef_u, coef_v, coef_w, orient, link):
    highest = lax.Precision.HIGHEST
    stacked = fields[0]
    layers_w = stacked.shape[1]
    rows_v = stacked.shape[2]
    rows_u = stacked.shape[3]
    columns_v = rows_v // RATIO + 4
    columns_u = rows_u // RATIO + 4
    moving = jnp.concatenate([stacked[0:3], stacked[4:7]], axis=0)
    low_u, high_u, coef_low_u, coef_high_u = neighbour_rows(moving, coef_u, "au", 3, 2)
    low_v, high_v, coef_low_v, coef_high_v = neighbour_rows(moving, coef_v, "vert", 2, 2)
    moving = moving.astype(jnp.float32)
    zero_w = jnp.zeros_like(moving[:, :2])
    slopes = (
        slopes_along(zero_w, moving, zero_w, 1),
        slopes_along(low_v, moving, high_v, 2),
        slopes_along(low_u, moving, high_u, 3),
    )
    product_sum = jnp.zeros(moving.shape[1:], jnp.float32)
    div_flow = jnp.zeros(moving.shape[1:], jnp.float32)
    div_adjoint = jnp.zeros(moving.shape[1:], jnp.float32)
    for direction, slope in enumerate(slopes):
        component = 2 - direction
        for k in range(3):
            product_sum = product_sum + slope[k] * slope[3 + k]
        div_flow = div_flow + slope[component]
        div_adjoint = div_adjoint + slope[3 + component]
    density = (
        product_sum
        - stacked[3].astype(jnp.float32) * div_adjoint
        - stacked[7].astype(jnp.float32) * div_flow
    )
    zero_coef = jnp.zeros_like(coef_w[:, :1])
    mat_w = smoothed_band(jnp.concatenate([zero_coef, coef_w, zero_coef], axis=1), layers_w // RATIO, 0)
    mat_v = smoothed_band(jnp.concatenate([coef_low_v, coef_v, coef_high_v], axis=1), columns_v, 2)
    mat_u = smoothed_band(jnp.concatenate([coef_low_u, coef_u, coef_high_u], axis=1), columns_u, 2)
    reduced = jnp.einsum("wvu,wa->avu", density, mat_w, precision=highest)
    reduced = fold_vert(jnp.einsum("avu,vb->abu", reduced, mat_v, precision=highest))
    reduced = fold_first(jnp.einsum("abu,uc->abc", reduced, mat_u, precision=highest))
    patch_index = lax.axis_index("patch")
    patches = lax.axis_size("patch")
    layers_d = reduced.shape[0]
    out_index = jnp.where(orient[patch_index, 0] == 1, 0, layers_d - 1).astype(jnp.int32)
    in_index = jnp.where(orient[patch_index, 1] == 1, layers_d - 1, 0).astype(jnp.int32)
    layer_ids = jnp.arange(layers_d)
    out_mask = (layer_ids == out_index).astype(jnp.float32)[:, None, None]
    in_mask = (layer_ids == in_index).astype(jnp.float32)[:, None, None]
    out_face = jnp.sum(out_mask * reduced, axis=0)
    in_face = jnp.sum(in_mask * reduced, axis=0)
    gate_here = link[patch_index].astype(jnp.float32)
    gate_before = link[(patch_index + patches - 1) % patches].astype(jnp.float32)
    from_before = from_behind(out_face * gate_here, "patch", 1)
    from_after = from_behind(in_face * gate_before, "patch", -1)
    design = reduced + in_mask * from_before[None] + out_mask * from_after[None]
    return design[None]


def solution(mesh):
    placed = (P("patch", None, None, "vert", "au"), P(None, "au"), P(None, "vert"), P(), P(), P())
    return jax.shard_map(
        shards,
        mesh=mesh,
        in_specs=placed,
        out_specs=P("patch", None, "vert", "au"),
        check_vma=False,
    )
```

```python
import numpy as np
import jax
import jax.numpy as jnp
from jax import lax
from jax.sharding import PartitionSpec as P

RATIO = 8


def with_halo(block, sides, width):
    for axis, dim in sides:
        count = lax.axis_size(axis)
        forward = [(i, i + 1) for i in range(count - 1)]
        backward = [(target, source) for source, target in forward]
        low = lax.ppermute(
            lax.slice_in_dim(block, block.shape[dim] - width, None, axis=dim), axis, forward
        )
        high = lax.ppermute(lax.slice_in_dim(block, 0, width, axis=dim), axis, backward)
        block = jnp.concatenate([low, block, high], axis=dim)
    return block


def from_behind(block, axis, distance):
    devices = range(lax.axis_size(axis))
    route = [((i - distance) % len(devices), i) for i in devices]
    return lax.ppermute(block, axis, route)


def field_density(extended, width, reach, layers_w, rows_v, rows_u):
    padded = jnp.pad(extended, ((0, 0), (2, 2), (0, 0), (0, 0)))
    channels = extended.shape[0]
    anchor = (0, 2, width - reach, width - reach)
    extent = (channels, layers_w, rows_v + 2 * reach, rows_u + 2 * reach)

    def shifted(direction, offset):
        corner_at = list(anchor)
        corner_at[direction] = corner_at[direction] + offset
        limit_at = tuple((b + s for b, s in zip(corner_at, extent)))
        return lax.slice(padded, tuple(corner_at), limit_at).astype(jnp.float32)

    centre = shifted(1, 0)
    product_sum = jnp.zeros(extent[1:], jnp.float32)
    div_flow = jnp.zeros(extent[1:], jnp.float32)
    div_adjoint = jnp.zeros(extent[1:], jnp.float32)
    for direction in (1, 2, 3):
        slopes = (
            8.0 * (shifted(direction, 1) - shifted(direction, -1))
            - (shifted(direction, 2) - shifted(direction, -2))
        ) / 12.0
        component = 3 - direction
        for k in range(3):
            product_sum = product_sum + slopes[k] * slopes[4 + k]
        div_flow = div_flow + slopes[component]
        div_adjoint = div_adjoint + slopes[4 + component]
    return product_sum - centre[3] * div_adjoint - centre[7] * div_flow


def blur(widened):
    padded = jnp.pad(widened, ((1, 1), (0, 0), (0, 0)))
    along_w = (padded[:-2] + 4.0 * padded[1:-1] + padded[2:]) / 6.0
    along_v = (along_w[:, :-2] + 4.0 * along_w[:, 1:-1] + along_w[:, 2:]) / 6.0
    return (along_v[:, :, :-2] + 4.0 * along_v[:, :, 1:-1] + along_v[:, :, 2:]) / 6.0


def band_matrix(coef_in, columns, offset):
    row_count = coef_in.shape[1]
    target = (jnp.arange(row_count) // RATIO)[:, None] + offset
    column = jnp.arange(columns)[None, :]
    result = jnp.zeros((row_count, columns), jnp.float32)
    for d in range(3):
        result = result + jnp.where(column == target + (d - 1), coef_in[d][:, None], 0.0)
    return result


def fold_vert(partial_value):
    widened = with_halo(partial_value, (("vert", 1),), 2)
    interior = widened[:, 4:-4]
    interior = interior.at[:, :2].add(widened[:, :2])
    return interior.at[:, -2:].add(widened[:, -2:])


def fold_first(partial_value):
    widened = with_halo(partial_value, (("au", 2),), 2)
    interior = widened[:, :, 4:-4]
    interior = interior.at[:, :, :2].add(widened[:, :, :2])
    return interior.at[:, :, -2:].add(widened[:, :, -2:])


def split_exact(vector):
    high = lax.reduce_precision(vector, exponent_bits=8, mantissa_bits=7)
    rest = vector - high
    middle = lax.reduce_precision(rest, exponent_bits=8, mantissa_bits=7)
    low = rest - middle
    return jnp.stack([high, middle, low]).astype(jnp.bfloat16)


def join_exact(parts):
    parts = parts.astype(jnp.float32)
    return parts[0] + (parts[1] + parts[2])


def spread_dim(piece):
    return piece.ndim - 1 if piece.shape[-1] >= 3 else piece.ndim - 2


def with_rider(piece, vector):
    parts = split_exact(vector)
    shape = (1,) + piece.shape[1:]
    spread = spread_dim(piece)
    assert shape[1] >= parts.shape[0] and shape[spread] >= parts.shape[1]
    grid = jnp.pad(parts, ((0, shape[1] - parts.shape[0]), (0, shape[spread] - parts.shape[1])))
    layout = [1] * piece.ndim
    layout[1] = shape[1]
    layout[spread] = shape[spread]
    slab = jnp.broadcast_to(grid.reshape(layout), shape)
    return jnp.concatenate([piece, slab], axis=0)


def neighbour_rows(stacked, coef, axis, dim, width):
    count = lax.axis_size(axis)
    forward = [(i, i + 1) for i in range(count - 1)]
    backward = [(target, source) for source, target in forward]
    length = stacked.shape[dim]
    low = lax.ppermute(
        with_rider(lax.slice_in_dim(stacked, length - width, None, axis=dim), coef[:, -1]), axis, forward
    )
    high = lax.ppermute(with_rider(lax.slice_in_dim(stacked, 0, width, axis=dim), coef[:, 0]), axis, backward)
    rider_at = [-1, slice(0, 3)] + [0] * (stacked.ndim - 2)
    rider_at[spread_dim(low)] = slice(0, coef.shape[0])
    rider_at = tuple(rider_at)
    coef_low = join_exact(low[rider_at])[:, None]
    coef_high = join_exact(high[rider_at])[:, None]
    return low[:-1], high[:-1], coef_low, coef_high


def slopes_along(low, core, high, dim):
    joined = jnp.concatenate([low.astype(jnp.float32), core, high.astype(jnp.float32)], axis=dim)
    length = core.shape[dim]

    def shifted(offset):
        return lax.slice_in_dim(joined, 2 + offset, 2 + offset + length, axis=dim)

    return (8.0 * (shifted(1) - shifted(-1)) - (shifted(2) - shifted(-2))) / 12.0


def smoothed_band(coef_ext, columns, offset):
    rows = coef_ext.shape[1] - 2
    target = np.floor_divide(np.arange(-1, rows + 1), RATIO)[:, None] + offset
    column = np.arange(columns)[None, :]
    band = jnp.zeros((rows + 2, columns), jnp.float32)
    for d in range(3):
        band = band + jnp.where(column == target + (d - 1), coef_ext[d][:, None], 0.0)
    return (band[:-2] + 4.0 * band[1:-1] + band[2:]) / 6.0


def shards(fields, coef_u, coef_v, coef_w, orient, link):
    highest = lax.Precision.HIGHEST
    stacked = fields[0]
    layers_w = stacked.shape[1]
    rows_v = stacked.shape[2]
    rows_u = stacked.shape[3]
    columns_v = rows_v // RATIO + 4
    columns_u = rows_u // RATIO + 4
    moving = jnp.concatenate([stacked[0:3], stacked[4:7]], axis=0)
    low_u, high_u, coef_low_u, coef_high_u = neighbour_rows(moving, coef_u, "au", 3, 2)
    low_v, high_v, coef_low_v, coef_high_v = neighbour_rows(moving, coef_v, "vert", 2, 2)
    moving = moving.astype(jnp.float32)
    zero_w = jnp.zeros_like(moving[:, :2])
    slopes = (
        slopes_along(zero_w, moving, zero_w, 1),
        slopes_along(low_v, moving, high_v, 2),
        slopes_along(low_u, moving, high_u, 3),
    )
    product_sum = jnp.zeros(moving.shape[1:], jnp.float32)
    div_flow = jnp.zeros(moving.shape[1:], jnp.float32)
    div_adjoint = jnp.zeros(moving.shape[1:], jnp.float32)
    for direction, slope in enumerate(slopes):
        component = 2 - direction
        for k in range(3):
            product_sum = product_sum + slope[k] * slope[3 + k]
        div_flow = div_flow + slope[component]
        div_adjoint = div_adjoint + slope[3 + component]
    density = (
        product_sum
        - stacked[3].astype(jnp.float32) * div_adjoint
        - stacked[7].astype(jnp.float32) * div_flow
    )
    zero_coef = jnp.zeros_like(coef_w[:, :1])
    mat_w = smoothed_band(jnp.concatenate([zero_coef, coef_w, zero_coef], axis=1), layers_w // RATIO, 0)
    mat_v = smoothed_band(jnp.concatenate([coef_low_v, coef_v, coef_high_v], axis=1), columns_v, 2)
    mat_u = smoothed_band(jnp.concatenate([coef_low_u, coef_u, coef_high_u], axis=1), columns_u, 2)
    reduced = jnp.einsum("wvu,wa->avu", density, mat_w, precision=highest)
    reduced = fold_vert(jnp.einsum("avu,vb->abu", reduced, mat_v, precision=highest))
    reduced = fold_first(jnp.einsum("abu,uc->abc", reduced, mat_u, precision=highest))
    patch_index = lax.axis_index("patch")
    patches = lax.axis_size("patch")
    layers_d = reduced.shape[0]
    ids = jnp.arange(patches)
    here = ids == patch_index
    before = ids == (patch_index + patches - 1) % patches
    orient_here = jnp.sum(jnp.where(here[:, None], orient, 0), axis=0, keepdims=True)
    out_index = jnp.where(orient_here[:, 0:1] == 1, 0, layers_d - 1)
    in_index = jnp.where(orient_here[:, 1:2] == 1, layers_d - 1, 0)
    layer_ids = jnp.arange(layers_d)[:, None]
    out_mask = (layer_ids == out_index).astype(jnp.float32)[:, :, None]
    in_mask = (layer_ids == in_index).astype(jnp.float32)[:, :, None]
    out_face = jnp.sum(out_mask * reduced, axis=0)
    in_face = jnp.sum(in_mask * reduced, axis=0)
    gate_here = jnp.sum(jnp.where(here, link, 0), keepdims=True).astype(jnp.float32)[:, None]
    gate_before = jnp.sum(jnp.where(before, link, 0), keepdims=True).astype(jnp.float32)[:, None]
    from_before = from_behind(out_face * gate_here, "patch", 1)
    from_after = from_behind(in_face * gate_before, "patch", -1)
    design = reduced + in_mask * from_before[None] + out_mask * from_after[None]
    return design[None]


def solution(mesh):
    placed = (P("patch", None, None, "vert", "au"), P(None, "au"), P(None, "vert"), P(), P(), P())
    return jax.shard_map(
        shards,
        mesh=mesh,
        in_specs=placed,
        out_specs=P("patch", None, "vert", "au"),
        check_vma=False,
    )
```

```python
import numpy as np
import jax
import jax.numpy as jnp
from jax import lax
from jax.sharding import PartitionSpec as P

RATIO = 8


def with_halo(block, sides, width):
    for axis, dim in sides:
        count = lax.axis_size(axis)
        forward = [(i, i + 1) for i in range(count - 1)]
        backward = [(target, source) for source, target in forward]
        low = lax.ppermute(
            lax.slice_in_dim(block, block.shape[dim] - width, None, axis=dim), axis, forward
        )
        high = lax.ppermute(lax.slice_in_dim(block, 0, width, axis=dim), axis, backward)
        block = jnp.concatenate([low, block, high], axis=dim)
    return block


def from_behind(block, axis, distance):
    devices = range(lax.axis_size(axis))
    route = [((i - distance) % len(devices), i) for i in devices]
    return lax.ppermute(block, axis, route)


def field_density(extended, width, reach, layers_w, rows_v, rows_u):
    padded = jnp.pad(extended, ((0, 0), (2, 2), (0, 0), (0, 0)))
    channels = extended.shape[0]
    anchor = (0, 2, width - reach, width - reach)
    extent = (channels, layers_w, rows_v + 2 * reach, rows_u + 2 * reach)

    def shifted(direction, offset):
        corner_at = list(anchor)
        corner_at[direction] = corner_at[direction] + offset
        limit_at = tuple((b + s for b, s in zip(corner_at, extent)))
        return lax.slice(padded, tuple(corner_at), limit_at).astype(jnp.float32)

    centre = shifted(1, 0)
    product_sum = jnp.zeros(extent[1:], jnp.float32)
    div_flow = jnp.zeros(extent[1:], jnp.float32)
    div_adjoint = jnp.zeros(extent[1:], jnp.float32)
    for direction in (1, 2, 3):
        slopes = (
            8.0 * (shifted(direction, 1) - shifted(direction, -1))
            - (shifted(direction, 2) - shifted(direction, -2))
        ) / 12.0
        component = 3 - direction
        for k in range(3):
            product_sum = product_sum + slopes[k] * slopes[4 + k]
        div_flow = div_flow + slopes[component]
        div_adjoint = div_adjoint + slopes[4 + component]
    return product_sum - centre[3] * div_adjoint - centre[7] * div_flow


def blur(widened):
    padded = jnp.pad(widened, ((1, 1), (0, 0), (0, 0)))
    along_w = (padded[:-2] + 4.0 * padded[1:-1] + padded[2:]) / 6.0
    along_v = (along_w[:, :-2] + 4.0 * along_w[:, 1:-1] + along_w[:, 2:]) / 6.0
    return (along_v[:, :, :-2] + 4.0 * along_v[:, :, 1:-1] + along_v[:, :, 2:]) / 6.0


def band_matrix(coef_in, columns, offset):
    row_count = coef_in.shape[1]
    target = (jnp.arange(row_count) // RATIO)[:, None] + offset
    column = jnp.arange(columns)[None, :]
    result = jnp.zeros((row_count, columns), jnp.float32)
    for d in range(3):
        result = result + jnp.where(column == target + (d - 1), coef_in[d][:, None], 0.0)
    return result


def fold_vert(partial_value):
    widened = with_halo(partial_value, (("vert", 1),), 2)
    interior = widened[:, 4:-4]
    interior = interior.at[:, :2].add(widened[:, :2])
    return interior.at[:, -2:].add(widened[:, -2:])


def fold_first(partial_value):
    widened = with_halo(partial_value, (("au", 2),), 2)
    interior = widened[:, :, 4:-4]
    interior = interior.at[:, :, :2].add(widened[:, :, :2])
    return interior.at[:, :, -2:].add(widened[:, :, -2:])


def split_exact(vector):
    high = lax.reduce_precision(vector, exponent_bits=8, mantissa_bits=7)
    rest = vector - high
    middle = lax.reduce_precision(rest, exponent_bits=8, mantissa_bits=7)
    low = rest - middle
    return jnp.stack([high, middle, low]).astype(jnp.bfloat16)


def join_exact(parts):
    parts = parts.astype(jnp.float32)
    return parts[0] + (parts[1] + parts[2])


def spread_dim(piece):
    return piece.ndim - 1 if piece.shape[-1] >= 3 else piece.ndim - 2


def with_rider(piece, vector):
    parts = split_exact(vector)
    shape = (1,) + piece.shape[1:]
    spread = spread_dim(piece)
    assert shape[1] >= parts.shape[0] and shape[spread] >= parts.shape[1]
    grid = jnp.pad(parts, ((0, shape[1] - parts.shape[0]), (0, shape[spread] - parts.shape[1])))
    layout = [1] * piece.ndim
    layout[1] = shape[1]
    layout[spread] = shape[spread]
    slab = jnp.broadcast_to(grid.reshape(layout), shape)
    return jnp.concatenate([piece, slab], axis=0)


def neighbour_rows(stacked, coef, axis, dim, width):
    count = lax.axis_size(axis)
    forward = [(i, i + 1) for i in range(count - 1)]
    backward = [(target, source) for source, target in forward]
    length = stacked.shape[dim]
    low = lax.ppermute(
        with_rider(lax.slice_in_dim(stacked, length - width, None, axis=dim), coef[:, -1]), axis, forward
    )
    high = lax.ppermute(with_rider(lax.slice_in_dim(stacked, 0, width, axis=dim), coef[:, 0]), axis, backward)
    rider_at = [-1, slice(0, 3)] + [0] * (stacked.ndim - 2)
    rider_at[spread_dim(low)] = slice(0, coef.shape[0])
    rider_at = tuple(rider_at)
    coef_low = join_exact(low[rider_at])[:, None]
    coef_high = join_exact(high[rider_at])[:, None]
    return low[:-1], high[:-1], coef_low, coef_high


def slopes_along(low, core, high, dim):
    joined = jnp.concatenate([low.astype(jnp.float32), core, high.astype(jnp.float32)], axis=dim)
    length = core.shape[dim]

    def shifted(offset):
        return lax.slice_in_dim(joined, 2 + offset, 2 + offset + length, axis=dim)

    return (8.0 * (shifted(1) - shifted(-1)) - (shifted(2) - shifted(-2))) / 12.0


def smoothed_band(coef_ext, columns, offset):
    rows = coef_ext.shape[1] - 2
    target = np.floor_divide(np.arange(-1, rows + 1), RATIO)[:, None] + offset
    column = np.arange(columns)[None, :]
    band = jnp.zeros((rows + 2, columns), jnp.float32)
    for d in range(3):
        band = band + jnp.where(column == target + (d - 1), coef_ext[d][:, None], 0.0)
    return (band[:-2] + 4.0 * band[1:-1] + band[2:]) / 6.0


def shards(fields, coef_u, coef_v, coef_w, orient, link):
    highest = lax.Precision.HIGHEST
    stacked = fields[0]
    layers_w = stacked.shape[1]
    rows_v = stacked.shape[2]
    rows_u = stacked.shape[3]
    columns_v = rows_v // RATIO + 4
    columns_u = rows_u // RATIO + 4
    moving = jnp.concatenate([stacked[0:3], stacked[4:7]], axis=0)
    low_u, high_u, coef_low_u, coef_high_u = neighbour_rows(moving, coef_u, "au", 3, 2)
    low_v, high_v, coef_low_v, coef_high_v = neighbour_rows(moving, coef_v, "vert", 2, 2)
    moving = moving.astype(jnp.float32)
    zero_w = jnp.zeros_like(moving[:, :2])
    slopes = (
        slopes_along(zero_w, moving, zero_w, 1),
        slopes_along(low_v, moving, high_v, 2),
        slopes_along(low_u, moving, high_u, 3),
    )
    product_sum = jnp.zeros(moving.shape[1:], jnp.float32)
    div_flow = jnp.zeros(moving.shape[1:], jnp.float32)
    div_adjoint = jnp.zeros(moving.shape[1:], jnp.float32)
    for direction, slope in enumerate(slopes):
        component = 2 - direction
        for k in range(3):
            product_sum = product_sum + slope[k] * slope[3 + k]
        div_flow = div_flow + slope[component]
        div_adjoint = div_adjoint + slope[3 + component]
    density = (
        product_sum
        - stacked[3].astype(jnp.float32) * div_adjoint
        - stacked[7].astype(jnp.float32) * div_flow
    )
    zero_coef = jnp.zeros_like(coef_w[:, :1])
    mat_w = smoothed_band(jnp.concatenate([zero_coef, coef_w, zero_coef], axis=1), layers_w // RATIO, 0)
    mat_v = smoothed_band(jnp.concatenate([coef_low_v, coef_v, coef_high_v], axis=1), columns_v, 2)
    mat_u = smoothed_band(jnp.concatenate([coef_low_u, coef_u, coef_high_u], axis=1), columns_u, 2)
    reduced = jnp.einsum("wvu,wa->avu", density, mat_w, precision=highest)
    reduced = fold_vert(jnp.einsum("avu,vb->abu", reduced, mat_v, precision=highest))
    reduced = fold_first(jnp.einsum("abu,uc->abc", reduced, mat_u, precision=highest))
    patch_index = lax.axis_index("patch")
    patches = lax.axis_size("patch")
    layers_d = reduced.shape[0]
    ids = jnp.arange(patches)[:, None]
    here = (ids == patch_index).astype(jnp.float32)
    before = (ids == (patch_index + patches - 1) % patches).astype(jnp.float32)
    layer_ids = jnp.arange(layers_d)[None, :]
    out_at = jnp.where(orient[:, 0:1] == 1, 0, layers_d - 1)
    in_at = jnp.where(orient[:, 1:2] == 1, layers_d - 1, 0)
    out_mask = jnp.sum(here * (layer_ids == out_at).astype(jnp.float32), axis=0)[:, None, None]
    in_mask = jnp.sum(here * (layer_ids == in_at).astype(jnp.float32), axis=0)[:, None, None]
    out_face = jnp.sum(out_mask * reduced, axis=0)
    in_face = jnp.sum(in_mask * reduced, axis=0)
    links = jnp.broadcast_to(link.astype(jnp.float32)[:, None, None], (patches,) + out_face.shape)
    gate_here = jnp.sum(here[:, :, None] * links, axis=0)
    gate_before = jnp.sum(before[:, :, None] * links, axis=0)
    from_before = from_behind(out_face * gate_here, "patch", 1)
    from_after = from_behind(in_face * gate_before, "patch", -1)
    design = reduced + in_mask * from_before[None] + out_mask * from_after[None]
    return design[None]


def solution(mesh):
    placed = (P("patch", None, None, "vert", "au"), P(None, "au"), P(None, "vert"), P(), P(), P())
    return jax.shard_map(
        shards,
        mesh=mesh,
        in_specs=placed,
        out_specs=P("patch", None, "vert", "au"),
        check_vma=False,
    )
```

```python
import numpy as np
import jax
import jax.numpy as jnp
from jax import lax
from jax.sharding import PartitionSpec as P

RATIO = 8


def with_halo(block, sides, width):
    for axis, dim in sides:
        count = lax.axis_size(axis)
        forward = [(i, i + 1) for i in range(count - 1)]
        backward = [(target, source) for source, target in forward]
        low = lax.ppermute(
            lax.slice_in_dim(block, block.shape[dim] - width, None, axis=dim), axis, forward
        )
        high = lax.ppermute(lax.slice_in_dim(block, 0, width, axis=dim), axis, backward)
        block = jnp.concatenate([low, block, high], axis=dim)
    return block


def from_behind(block, axis, distance):
    devices = range(lax.axis_size(axis))
    route = [((i - distance) % len(devices), i) for i in devices]
    return lax.ppermute(block, axis, route)


def field_density(extended, width, reach, layers_w, rows_v, rows_u):
    padded = jnp.pad(extended, ((0, 0), (2, 2), (0, 0), (0, 0)))
    channels = extended.shape[0]
    anchor = (0, 2, width - reach, width - reach)
    extent = (channels, layers_w, rows_v + 2 * reach, rows_u + 2 * reach)

    def shifted(direction, offset):
        corner_at = list(anchor)
        corner_at[direction] = corner_at[direction] + offset
        limit_at = tuple((b + s for b, s in zip(corner_at, extent)))
        return lax.slice(padded, tuple(corner_at), limit_at).astype(jnp.float32)

    centre = shifted(1, 0)
    product_sum = jnp.zeros(extent[1:], jnp.float32)
    div_flow = jnp.zeros(extent[1:], jnp.float32)
    div_adjoint = jnp.zeros(extent[1:], jnp.float32)
    for direction in (1, 2, 3):
        slopes = (
            8.0 * (shifted(direction, 1) - shifted(direction, -1))
            - (shifted(direction, 2) - shifted(direction, -2))
        ) / 12.0
        component = 3 - direction
        for k in range(3):
            product_sum = product_sum + slopes[k] * slopes[4 + k]
        div_flow = div_flow + slopes[component]
        div_adjoint = div_adjoint + slopes[4 + component]
    return product_sum - centre[3] * div_adjoint - centre[7] * div_flow


def blur(widened):
    padded = jnp.pad(widened, ((1, 1), (0, 0), (0, 0)))
    along_w = (padded[:-2] + 4.0 * padded[1:-1] + padded[2:]) / 6.0
    along_v = (along_w[:, :-2] + 4.0 * along_w[:, 1:-1] + along_w[:, 2:]) / 6.0
    return (along_v[:, :, :-2] + 4.0 * along_v[:, :, 1:-1] + along_v[:, :, 2:]) / 6.0


def band_matrix(coef_in, columns, offset):
    row_count = coef_in.shape[1]
    target = (jnp.arange(row_count) // RATIO)[:, None] + offset
    column = jnp.arange(columns)[None, :]
    result = jnp.zeros((row_count, columns), jnp.float32)
    for d in range(3):
        result = result + jnp.where(column == target + (d - 1), coef_in[d][:, None], 0.0)
    return result


def fold_along(partial_value, axis, dim):
    widened = with_halo(partial_value, ((axis, dim),), 2)
    length = widened.shape[dim]
    interior = lax.slice_in_dim(widened, 4, length - 4, axis=dim)
    inner = interior.shape[dim]
    widths = [(0, 0)] * widened.ndim
    widths[dim] = (0, inner - 2)
    from_low = jnp.pad(lax.slice_in_dim(widened, 0, 2, axis=dim), widths)
    widths[dim] = (inner - 2, 0)
    from_high = jnp.pad(lax.slice_in_dim(widened, length - 2, length, axis=dim), widths)
    return interior + from_low + from_high


def fold_vert(partial_value):
    return fold_along(partial_value, "vert", 1)


def fold_first(partial_value):
    return fold_along(partial_value, "au", 2)


def split_exact(vector):
    high = lax.reduce_precision(vector, exponent_bits=8, mantissa_bits=7)
    rest = vector - high
    middle = lax.reduce_precision(rest, exponent_bits=8, mantissa_bits=7)
    low = rest - middle
    return jnp.stack([high, middle, low]).astype(jnp.bfloat16)


def join_exact(parts):
    parts = parts.astype(jnp.float32)
    return parts[0] + (parts[1] + parts[2])


def spread_dim(piece):
    return piece.ndim - 1 if piece.shape[-1] >= 3 else piece.ndim - 2


def with_rider(piece, vector):
    parts = split_exact(vector)
    shape = (1,) + piece.shape[1:]
    spread = spread_dim(piece)
    assert shape[1] >= parts.shape[0] and shape[spread] >= parts.shape[1]
    grid = jnp.pad(parts, ((0, shape[1] - parts.shape[0]), (0, shape[spread] - parts.shape[1])))
    layout = [1] * piece.ndim
    layout[1] = shape[1]
    layout[spread] = shape[spread]
    slab = jnp.broadcast_to(grid.reshape(layout), shape)
    return jnp.concatenate([piece, slab], axis=0)


def neighbour_rows(stacked, coef, axis, dim, width):
    count = lax.axis_size(axis)
    forward = [(i, i + 1) for i in range(count - 1)]
    backward = [(target, source) for source, target in forward]
    length = stacked.shape[dim]
    low = lax.ppermute(
        with_rider(lax.slice_in_dim(stacked, length - width, None, axis=dim), coef[:, -1]), axis, forward
    )
    high = lax.ppermute(with_rider(lax.slice_in_dim(stacked, 0, width, axis=dim), coef[:, 0]), axis, backward)
    rider_at = [-1, slice(0, 3)] + [0] * (stacked.ndim - 2)
    rider_at[spread_dim(low)] = slice(0, coef.shape[0])
    rider_at = tuple(rider_at)
    coef_low = join_exact(low[rider_at])[:, None]
    coef_high = join_exact(high[rider_at])[:, None]
    return low[:-1], high[:-1], coef_low, coef_high


def slopes_along(low, core, high, dim):
    joined = jnp.concatenate([low.astype(jnp.float32), core, high.astype(jnp.float32)], axis=dim)
    length = core.shape[dim]

    def shifted(offset):
        return lax.slice_in_dim(joined, 2 + offset, 2 + offset + length, axis=dim)

    return (8.0 * (shifted(1) - shifted(-1)) - (shifted(2) - shifted(-2))) / 12.0


def smoothed_band(coef_ext, columns, offset):
    rows = coef_ext.shape[1] - 2
    target = np.floor_divide(np.arange(-1, rows + 1), RATIO)[:, None] + offset
    column = np.arange(columns)[None, :]
    band = jnp.zeros((rows + 2, columns), jnp.float32)
    for d in range(3):
        band = band + jnp.where(column == target + (d - 1), coef_ext[d][:, None], 0.0)
    return (band[:-2] + 4.0 * band[1:-1] + band[2:]) / 6.0


def shards(fields, coef_u, coef_v, coef_w, orient, link):
    highest = lax.Precision.HIGHEST
    stacked = fields[0]
    layers_w = stacked.shape[1]
    rows_v = stacked.shape[2]
    rows_u = stacked.shape[3]
    columns_v = rows_v // RATIO + 4
    columns_u = rows_u // RATIO + 4
    moving = jnp.concatenate([stacked[0:3], stacked[4:7]], axis=0)
    low_u, high_u, coef_low_u, coef_high_u = neighbour_rows(moving, coef_u, "au", 3, 2)
    low_v, high_v, coef_low_v, coef_high_v = neighbour_rows(moving, coef_v, "vert", 2, 2)
    moving = moving.astype(jnp.float32)
    zero_w = jnp.zeros_like(moving[:, :2])
    slopes = (
        slopes_along(zero_w, moving, zero_w, 1),
        slopes_along(low_v, moving, high_v, 2),
        slopes_along(low_u, moving, high_u, 3),
    )
    product_sum = jnp.zeros(moving.shape[1:], jnp.float32)
    div_flow = jnp.zeros(moving.shape[1:], jnp.float32)
    div_adjoint = jnp.zeros(moving.shape[1:], jnp.float32)
    for direction, slope in enumerate(slopes):
        component = 2 - direction
        for k in range(3):
            product_sum = product_sum + slope[k] * slope[3 + k]
        div_flow = div_flow + slope[component]
        div_adjoint = div_adjoint + slope[3 + component]
    density = (
        product_sum
        - stacked[3].astype(jnp.float32) * div_adjoint
        - stacked[7].astype(jnp.float32) * div_flow
    )
    zero_coef = jnp.zeros_like(coef_w[:, :1])
    mat_w = smoothed_band(jnp.concatenate([zero_coef, coef_w, zero_coef], axis=1), layers_w // RATIO, 0)
    mat_v = smoothed_band(jnp.concatenate([coef_low_v, coef_v, coef_high_v], axis=1), columns_v, 2)
    mat_u = smoothed_band(jnp.concatenate([coef_low_u, coef_u, coef_high_u], axis=1), columns_u, 2)
    reduced = jnp.einsum("wvu,wa->avu", density, mat_w, precision=highest)
    reduced = fold_vert(jnp.einsum("avu,vb->abu", reduced, mat_v, precision=highest))
    reduced = fold_first(jnp.einsum("abu,uc->abc", reduced, mat_u, precision=highest))
    patch_index = lax.axis_index("patch")
    patches = lax.axis_size("patch")
    layers_d = reduced.shape[0]
    out_index = jnp.where(orient[patch_index, 0] == 1, 0, layers_d - 1).astype(jnp.int32)
    in_index = jnp.where(orient[patch_index, 1] == 1, layers_d - 1, 0).astype(jnp.int32)
    layer_ids = jnp.arange(layers_d)
    out_mask = (layer_ids == out_index).astype(jnp.float32)[:, None, None]
    in_mask = (layer_ids == in_index).astype(jnp.float32)[:, None, None]
    out_face = jnp.sum(out_mask * reduced, axis=0)
    in_face = jnp.sum(in_mask * reduced, axis=0)
    gate_here = link[patch_index].astype(jnp.float32)
    gate_before = link[(patch_index + patches - 1) % patches].astype(jnp.float32)
    from_before = from_behind(out_face * gate_here, "patch", 1)
    from_after = from_behind(in_face * gate_before, "patch", -1)
    design = reduced + in_mask * from_before[None] + out_mask * from_after[None]
    return design[None]


def solution(mesh):
    placed = (P("patch", None, None, "vert", "au"), P(None, "au"), P(None, "vert"), P(), P(), P())
    return jax.shard_map(
        shards,
        mesh=mesh,
        in_specs=placed,
        out_specs=P("patch", None, "vert", "au"),
        check_vma=False,
    )
```

```python
import numpy as np
import jax
import jax.numpy as jnp
from jax import lax
from jax.sharding import PartitionSpec as P

RATIO = 8


def with_halo(block, sides, width):
    for axis, dim in sides:
        count = lax.axis_size(axis)
        forward = [(i, i + 1) for i in range(count - 1)]
        backward = [(target, source) for source, target in forward]
        low = lax.ppermute(
            lax.slice_in_dim(block, block.shape[dim] - width, None, axis=dim), axis, forward
        )
        high = lax.ppermute(lax.slice_in_dim(block, 0, width, axis=dim), axis, backward)
        block = jnp.concatenate([low, block, high], axis=dim)
    return block


def from_behind(block, axis, distance):
    devices = range(lax.axis_size(axis))
    route = [((i - distance) % len(devices), i) for i in devices]
    return lax.ppermute(block, axis, route)


def field_density(extended, width, reach, layers_w, rows_v, rows_u):
    padded = jnp.pad(extended, ((0, 0), (2, 2), (0, 0), (0, 0)))
    channels = extended.shape[0]
    anchor = (0, 2, width - reach, width - reach)
    extent = (channels, layers_w, rows_v + 2 * reach, rows_u + 2 * reach)

    def shifted(direction, offset):
        corner_at = list(anchor)
        corner_at[direction] = corner_at[direction] + offset
        limit_at = tuple((b + s for b, s in zip(corner_at, extent)))
        return lax.slice(padded, tuple(corner_at), limit_at).astype(jnp.float32)

    centre = shifted(1, 0)
    product_sum = jnp.zeros(extent[1:], jnp.float32)
    div_flow = jnp.zeros(extent[1:], jnp.float32)
    div_adjoint = jnp.zeros(extent[1:], jnp.float32)
    for direction in (1, 2, 3):
        slopes = (
            8.0 * (shifted(direction, 1) - shifted(direction, -1))
            - (shifted(direction, 2) - shifted(direction, -2))
        ) / 12.0
        component = 3 - direction
        for k in range(3):
            product_sum = product_sum + slopes[k] * slopes[4 + k]
        div_flow = div_flow + slopes[component]
        div_adjoint = div_adjoint + slopes[4 + component]
    return product_sum - centre[3] * div_adjoint - centre[7] * div_flow


def blur(widened):
    padded = jnp.pad(widened, ((1, 1), (0, 0), (0, 0)))
    along_w = (padded[:-2] + 4.0 * padded[1:-1] + padded[2:]) / 6.0
    along_v = (along_w[:, :-2] + 4.0 * along_w[:, 1:-1] + along_w[:, 2:]) / 6.0
    return (along_v[:, :, :-2] + 4.0 * along_v[:, :, 1:-1] + along_v[:, :, 2:]) / 6.0


def band_matrix(coef_in, columns, offset):
    row_count = coef_in.shape[1]
    target = (jnp.arange(row_count) // RATIO)[:, None] + offset
    column = jnp.arange(columns)[None, :]
    result = jnp.zeros((row_count, columns), jnp.float32)
    for d in range(3):
        result = result + jnp.where(column == target + (d - 1), coef_in[d][:, None], 0.0)
    return result


def fold_along(partial_value, axis, dim):
    widened = with_halo(partial_value, ((axis, dim),), 2)
    length = widened.shape[dim]
    interior = lax.slice_in_dim(widened, 4, length - 4, axis=dim)
    inner = interior.shape[dim]
    widths = [(0, 0)] * widened.ndim
    widths[dim] = (0, inner - 2)
    from_low = jnp.pad(lax.slice_in_dim(widened, 0, 2, axis=dim), widths)
    widths[dim] = (inner - 2, 0)
    from_high = jnp.pad(lax.slice_in_dim(widened, length - 2, length, axis=dim), widths)
    return interior + from_low + from_high


def fold_vert(partial_value):
    return fold_along(partial_value, "vert", 1)


def fold_first(partial_value):
    return fold_along(partial_value, "au", 2)


def split_exact(vector):
    high = lax.reduce_precision(vector, exponent_bits=8, mantissa_bits=7)
    rest = vector - high
    middle = lax.reduce_precision(rest, exponent_bits=8, mantissa_bits=7)
    low = rest - middle
    return jnp.stack([high, middle, low]).astype(jnp.bfloat16)


def join_exact(parts):
    parts = parts.astype(jnp.float32)
    return parts[0] + (parts[1] + parts[2])


def spread_dim(piece):
    return piece.ndim - 1 if piece.shape[-1] >= 3 else piece.ndim - 2


def with_rider(piece, vector):
    parts = split_exact(vector)
    shape = (1,) + piece.shape[1:]
    spread = spread_dim(piece)
    assert shape[1] >= parts.shape[0] and shape[spread] >= parts.shape[1]
    grid = jnp.pad(parts, ((0, shape[1] - parts.shape[0]), (0, shape[spread] - parts.shape[1])))
    layout = [1] * piece.ndim
    layout[1] = shape[1]
    layout[spread] = shape[spread]
    slab = jnp.broadcast_to(grid.reshape(layout), shape)
    return jnp.concatenate([piece, slab], axis=0)


def neighbour_rows(stacked, coef, axis, dim, width):
    count = lax.axis_size(axis)
    forward = [(i, i + 1) for i in range(count - 1)]
    backward = [(target, source) for source, target in forward]
    length = stacked.shape[dim]
    low = lax.ppermute(
        with_rider(lax.slice_in_dim(stacked, length - width, None, axis=dim), coef[:, -1]), axis, forward
    )
    high = lax.ppermute(with_rider(lax.slice_in_dim(stacked, 0, width, axis=dim), coef[:, 0]), axis, backward)
    rider_at = [-1, slice(0, 3)] + [0] * (stacked.ndim - 2)
    rider_at[spread_dim(low)] = slice(0, coef.shape[0])
    rider_at = tuple(rider_at)
    coef_low = join_exact(low[rider_at])[:, None]
    coef_high = join_exact(high[rider_at])[:, None]
    return low[:-1], high[:-1], coef_low, coef_high


def slopes_along(low, core, high, dim):
    joined = jnp.concatenate([low.astype(jnp.float32), core, high.astype(jnp.float32)], axis=dim)
    length = core.shape[dim]

    def shifted(offset):
        return lax.slice_in_dim(joined, 2 + offset, 2 + offset + length, axis=dim)

    return (8.0 * (shifted(1) - shifted(-1)) - (shifted(2) - shifted(-2))) / 12.0


def smoothed_band(coef_ext, columns, offset):
    rows = coef_ext.shape[1] - 2
    target = np.floor_divide(np.arange(-1, rows + 1), RATIO)[:, None] + offset
    column = np.arange(columns)[None, :]
    band = jnp.zeros((rows + 2, columns), jnp.float32)
    for d in range(3):
        band = band + jnp.where(column == target + (d - 1), coef_ext[d][:, None], 0.0)
    return (band[:-2] + 4.0 * band[1:-1] + band[2:]) / 6.0


def shards(fields, coef_u, coef_v, coef_w, orient, link):
    highest = lax.Precision.HIGHEST
    stacked = fields[0]
    layers_w = stacked.shape[1]
    rows_v = stacked.shape[2]
    rows_u = stacked.shape[3]
    columns_v = rows_v // RATIO + 4
    columns_u = rows_u // RATIO + 4
    moving = jnp.concatenate([stacked[0:3], stacked[4:7]], axis=0)
    low_u, high_u, coef_low_u, coef_high_u = neighbour_rows(moving, coef_u, "au", 3, 2)
    low_v, high_v, coef_low_v, coef_high_v = neighbour_rows(moving, coef_v, "vert", 2, 2)
    moving = moving.astype(jnp.float32)
    zero_w = jnp.zeros_like(moving[:, :2])
    slopes = (
        slopes_along(zero_w, moving, zero_w, 1),
        slopes_along(low_v, moving, high_v, 2),
        slopes_along(low_u, moving, high_u, 3),
    )
    product_sum = jnp.zeros(moving.shape[1:], jnp.float32)
    div_flow = jnp.zeros(moving.shape[1:], jnp.float32)
    div_adjoint = jnp.zeros(moving.shape[1:], jnp.float32)
    for direction, slope in enumerate(slopes):
        component = 2 - direction
        for k in range(3):
            product_sum = product_sum + slope[k] * slope[3 + k]
        div_flow = div_flow + slope[component]
        div_adjoint = div_adjoint + slope[3 + component]
    density = (
        product_sum
        - stacked[3].astype(jnp.float32) * div_adjoint
        - stacked[7].astype(jnp.float32) * div_flow
    )
    zero_coef = jnp.zeros_like(coef_w[:, :1])
    mat_w = smoothed_band(jnp.concatenate([zero_coef, coef_w, zero_coef], axis=1), layers_w // RATIO, 0)
    mat_v = smoothed_band(jnp.concatenate([coef_low_v, coef_v, coef_high_v], axis=1), columns_v, 2)
    mat_u = smoothed_band(jnp.concatenate([coef_low_u, coef_u, coef_high_u], axis=1), columns_u, 2)
    reduced = jnp.einsum("wvu,wa->avu", density, mat_w, precision=highest)
    reduced = fold_vert(jnp.einsum("avu,vb->abu", reduced, mat_v, precision=highest))
    reduced = fold_first(jnp.einsum("abu,uc->abc", reduced, mat_u, precision=highest))
    patch_index = lax.axis_index("patch")
    patches = lax.axis_size("patch")
    layers_d = reduced.shape[0]
    out_index = jnp.where(orient[patch_index, 0] == 1, 0, layers_d - 1).astype(jnp.int32)
    in_index = jnp.where(orient[patch_index, 1] == 1, layers_d - 1, 0).astype(jnp.int32)
    layer_ids = jnp.arange(layers_d)
    out_mask = (layer_ids == out_index).astype(jnp.float32)[:, None, None]
    in_mask = (layer_ids == in_index).astype(jnp.float32)[:, None, None]
    out_face = jnp.sum(out_mask * reduced, axis=0)
    in_face = jnp.sum(in_mask * reduced, axis=0)
    gate_here = link[patch_index].astype(jnp.float32)
    gate_before = link[(patch_index + patches - 1) % patches].astype(jnp.float32)
    from_before = from_behind(out_face * gate_here, "patch", 1)
    from_after = from_behind(in_face * gate_before, "patch", -1)
    rows = [
        reduced[layer] + in_mask[layer] * from_before + out_mask[layer] * from_after
        for layer in range(layers_d)
    ]
    return jnp.stack(rows)[None]


def solution(mesh):
    placed = (P("patch", None, None, "vert", "au"), P(None, "au"), P(None, "vert"), P(), P(), P())
    return jax.shard_map(
        shards,
        mesh=mesh,
        in_specs=placed,
        out_specs=P("patch", None, "vert", "au"),
        check_vma=False,
    )
```

```python
import numpy as np
import jax
import jax.numpy as jnp
from jax import lax
from jax.sharding import PartitionSpec as P

RATIO = 8


def with_halo(block, sides, width):
    for axis, dim in sides:
        count = lax.axis_size(axis)
        forward = [(i, i + 1) for i in range(count - 1)]
        backward = [(target, source) for source, target in forward]
        low = lax.ppermute(
            lax.slice_in_dim(block, block.shape[dim] - width, None, axis=dim), axis, forward
        )
        high = lax.ppermute(lax.slice_in_dim(block, 0, width, axis=dim), axis, backward)
        block = jnp.concatenate([low, block, high], axis=dim)
    return block


def from_behind(block, axis, distance):
    devices = range(lax.axis_size(axis))
    route = [((i - distance) % len(devices), i) for i in devices]
    return lax.ppermute(block, axis, route)


def field_density(extended, width, reach, layers_w, rows_v, rows_u):
    padded = jnp.pad(extended, ((0, 0), (2, 2), (0, 0), (0, 0)))
    channels = extended.shape[0]
    anchor = (0, 2, width - reach, width - reach)
    extent = (channels, layers_w, rows_v + 2 * reach, rows_u + 2 * reach)

    def shifted(direction, offset):
        corner_at = list(anchor)
        corner_at[direction] = corner_at[direction] + offset
        limit_at = tuple((b + s for b, s in zip(corner_at, extent)))
        return lax.slice(padded, tuple(corner_at), limit_at).astype(jnp.float32)

    centre = shifted(1, 0)
    product_sum = jnp.zeros(extent[1:], jnp.float32)
    div_flow = jnp.zeros(extent[1:], jnp.float32)
    div_adjoint = jnp.zeros(extent[1:], jnp.float32)
    for direction in (1, 2, 3):
        slopes = (
            8.0 * (shifted(direction, 1) - shifted(direction, -1))
            - (shifted(direction, 2) - shifted(direction, -2))
        ) / 12.0
        component = 3 - direction
        for k in range(3):
            product_sum = product_sum + slopes[k] * slopes[4 + k]
        div_flow = div_flow + slopes[component]
        div_adjoint = div_adjoint + slopes[4 + component]
    return product_sum - centre[3] * div_adjoint - centre[7] * div_flow


def blur(widened):
    padded = jnp.pad(widened, ((1, 1), (0, 0), (0, 0)))
    along_w = (padded[:-2] + 4.0 * padded[1:-1] + padded[2:]) / 6.0
    along_v = (along_w[:, :-2] + 4.0 * along_w[:, 1:-1] + along_w[:, 2:]) / 6.0
    return (along_v[:, :, :-2] + 4.0 * along_v[:, :, 1:-1] + along_v[:, :, 2:]) / 6.0


def band_matrix(coef_in, columns, offset):
    row_count = coef_in.shape[1]
    target = (jnp.arange(row_count) // RATIO)[:, None] + offset
    column = jnp.arange(columns)[None, :]
    result = jnp.zeros((row_count, columns), jnp.float32)
    for d in range(3):
        result = result + jnp.where(column == target + (d - 1), coef_in[d][:, None], 0.0)
    return result


def fold_along(partial_value, axis, dim):
    widened = with_halo(partial_value, ((axis, dim),), 2)
    length = widened.shape[dim]
    interior = lax.slice_in_dim(widened, 4, length - 4, axis=dim)
    inner = interior.shape[dim]
    widths = [(0, 0)] * widened.ndim
    widths[dim] = (0, inner - 2)
    from_low = jnp.pad(lax.slice_in_dim(widened, 0, 2, axis=dim), widths)
    widths[dim] = (inner - 2, 0)
    from_high = jnp.pad(lax.slice_in_dim(widened, length - 2, length, axis=dim), widths)
    return interior + from_low + from_high


def fold_vert(partial_value):
    return fold_along(partial_value, "vert", 1)


def fold_first(partial_value):
    return fold_along(partial_value, "au", 2)


def split_exact(vector):
    high = lax.reduce_precision(vector, exponent_bits=8, mantissa_bits=7)
    rest = vector - high
    middle = lax.reduce_precision(rest, exponent_bits=8, mantissa_bits=7)
    low = rest - middle
    return jnp.stack([high, middle, low]).astype(jnp.bfloat16)


def join_exact(parts):
    parts = parts.astype(jnp.float32)
    return parts[0] + (parts[1] + parts[2])


def spread_dim(piece):
    return piece.ndim - 1 if piece.shape[-1] >= 3 else piece.ndim - 2


def with_rider(piece, vector):
    parts = split_exact(vector)
    shape = (1,) + piece.shape[1:]
    spread = spread_dim(piece)
    assert shape[1] >= parts.shape[0] and shape[spread] >= parts.shape[1]
    grid = jnp.pad(parts, ((0, shape[1] - parts.shape[0]), (0, shape[spread] - parts.shape[1])))
    layout = [1] * piece.ndim
    layout[1] = shape[1]
    layout[spread] = shape[spread]
    slab = jnp.broadcast_to(grid.reshape(layout), shape)
    return jnp.concatenate([piece, slab], axis=0)


def neighbour_rows(stacked, coef, axis, dim, width):
    count = lax.axis_size(axis)
    forward = [(i, i + 1) for i in range(count - 1)]
    backward = [(target, source) for source, target in forward]
    length = stacked.shape[dim]
    low = lax.ppermute(
        with_rider(lax.slice_in_dim(stacked, length - width, None, axis=dim), coef[:, -1]), axis, forward
    )
    high = lax.ppermute(with_rider(lax.slice_in_dim(stacked, 0, width, axis=dim), coef[:, 0]), axis, backward)
    rider_at = [-1, slice(0, 3)] + [0] * (stacked.ndim - 2)
    rider_at[spread_dim(low)] = slice(0, coef.shape[0])
    rider_at = tuple(rider_at)
    coef_low = join_exact(low[rider_at])[:, None]
    coef_high = join_exact(high[rider_at])[:, None]
    return low[:-1], high[:-1], coef_low, coef_high


def slopes_along(low, core, high, dim):
    joined = jnp.concatenate([low.astype(jnp.float32), core, high.astype(jnp.float32)], axis=dim)
    length = core.shape[dim]

    def shifted(offset):
        return lax.slice_in_dim(joined, 2 + offset, 2 + offset + length, axis=dim)

    return (8.0 * (shifted(1) - shifted(-1)) - (shifted(2) - shifted(-2))) / 12.0


def smoothed_band(coef_ext, columns, offset):
    rows = coef_ext.shape[1] - 2
    target = np.floor_divide(np.arange(-1, rows + 1), RATIO)[:, None] + offset
    column = np.arange(columns)[None, :]
    band = jnp.zeros((rows + 2, columns), jnp.float32)
    for d in range(3):
        band = band + jnp.where(column == target + (d - 1), coef_ext[d][:, None], 0.0)
    return (band[:-2] + 4.0 * band[1:-1] + band[2:]) / 6.0


def shards(fields, coef_u, coef_v, coef_w, orient, link):
    highest = lax.Precision.HIGHEST
    stacked = fields[0]
    layers_w = stacked.shape[1]
    rows_v = stacked.shape[2]
    rows_u = stacked.shape[3]
    columns_v = rows_v // RATIO + 4
    columns_u = rows_u // RATIO + 4
    moving = jnp.concatenate([stacked[0:3], stacked[4:7]], axis=0)
    low_u, high_u, coef_low_u, coef_high_u = neighbour_rows(moving, coef_u, "au", 3, 2)
    low_v, high_v, coef_low_v, coef_high_v = neighbour_rows(moving, coef_v, "vert", 2, 2)
    moving = moving.astype(jnp.float32)
    zero_w = jnp.zeros_like(moving[:, :2])
    slopes = (
        slopes_along(zero_w, moving, zero_w, 1),
        slopes_along(low_v, moving, high_v, 2),
        slopes_along(low_u, moving, high_u, 3),
    )
    product_sum = jnp.zeros(moving.shape[1:], jnp.float32)
    div_flow = jnp.zeros(moving.shape[1:], jnp.float32)
    div_adjoint = jnp.zeros(moving.shape[1:], jnp.float32)
    for direction, slope in enumerate(slopes):
        component = 2 - direction
        for k in range(3):
            product_sum = product_sum + slope[k] * slope[3 + k]
        div_flow = div_flow + slope[component]
        div_adjoint = div_adjoint + slope[3 + component]
    density = (
        product_sum
        - stacked[3].astype(jnp.float32) * div_adjoint
        - stacked[7].astype(jnp.float32) * div_flow
    )
    zero_coef = jnp.zeros_like(coef_w[:, :1])
    mat_w = smoothed_band(jnp.concatenate([zero_coef, coef_w, zero_coef], axis=1), layers_w // RATIO, 0)
    mat_v = smoothed_band(jnp.concatenate([coef_low_v, coef_v, coef_high_v], axis=1), columns_v, 2)
    mat_u = smoothed_band(jnp.concatenate([coef_low_u, coef_u, coef_high_u], axis=1), columns_u, 2)
    reduced = jnp.einsum("wvu,wa->avu", density, mat_w, precision=highest)
    reduced = jnp.einsum("avu,uc->avc", reduced, mat_u, precision=highest)
    reduced = fold_vert(jnp.einsum("avc,vb->abc", reduced, mat_v, precision=highest))
    reduced = fold_first(reduced)
    patch_index = lax.axis_index("patch")
    patches = lax.axis_size("patch")
    layers_d = reduced.shape[0]
    out_index = jnp.where(orient[patch_index, 0] == 1, 0, layers_d - 1).astype(jnp.int32)
    in_index = jnp.where(orient[patch_index, 1] == 1, layers_d - 1, 0).astype(jnp.int32)
    layer_ids = jnp.arange(layers_d)
    out_mask = (layer_ids == out_index).astype(jnp.float32)[:, None, None]
    in_mask = (layer_ids == in_index).astype(jnp.float32)[:, None, None]
    out_face = jnp.sum(out_mask * reduced, axis=0)
    in_face = jnp.sum(in_mask * reduced, axis=0)
    gate_here = link[patch_index].astype(jnp.float32)
    gate_before = link[(patch_index + patches - 1) % patches].astype(jnp.float32)
    from_before = from_behind(out_face * gate_here, "patch", 1)
    from_after = from_behind(in_face * gate_before, "patch", -1)
    design = reduced + in_mask * from_before[None] + out_mask * from_after[None]
    return design[None]


def solution(mesh):
    placed = (P("patch", None, None, "vert", "au"), P(None, "au"), P(None, "vert"), P(), P(), P())
    return jax.shard_map(
        shards,
        mesh=mesh,
        in_specs=placed,
        out_specs=P("patch", None, "vert", "au"),
        check_vma=False,
    )
```
